32 devices in a mesh: req: 8 (over y, x, core), tp: 4 (over z).
Axes of the slice: x: 2, y: 2, z: 4, core: 2. Of those that a mesh axis runs over, the one named last changes fastest.
Arguments:
- queries: bfloat16 [1536, 2560], P('req', 'tp'), may hold values from -5 to 5
- new_keys: bfloat16 [1536, 512], P('req', 'tp'), may hold values from -5 to 5
- new_values: bfloat16 [1536, 512], P('req', 'tp'), may hold values from -5 to 5
- key_pages: bfloat16 [512, 64, 512], P('req', None, 'tp'), may hold values from -5 to 5
- value_pages: bfloat16 [512, 64, 512], P('req', None, 'tp'), may hold values from -5 to 5
- page_table: int32 [32, 16], P('req'), may hold values from 0 to 511, as said below
- cache_lengths: int32 [32], P('req'), may hold values from 2 to 1024, as said below
- parents: int32 [32, 48], P('req'), may hold values from -1 to 46, as said below
- residual: bfloat16 [1536, 2560], P('req'), may hold values from -6 to 6
- out_weight: bfloat16 [2560, 2560], P('tp'), may hold values from -0.125 to 0.125
- norm_gain: float32 [2560], replicated, may hold values from 0.1 to 1.9
- router_weight: float32 [2560, 16], replicated, may hold values from -0.125 to 0.125
- routes: int32 [1536, 6], P('req'), may hold values from 0 to 15, all different within a row; in each aligned block of 192 rows (0 to 191, 192 to 383, ...) at most 91 rows name the same one
- expert_gate_up: bfloat16 [16, 2560, 2, 1536], P('req', None, None, 'tp'), may hold values from -0.125 to 0.125
- expert_down: bfloat16 [16, 1536, 2560], P('req', 'tp'), may hold values from -0.15625 to 0.15625
- shared_gate_up: bfloat16 [2560, 2, 1536], P(None, None, 'tp'), may hold values from -0.125 to 0.125
- shared_down: bfloat16 [1536, 2560], P('tp'), may hold values from -0.15625 to 0.15625
Outputs:
- layer_out: bfloat16 [1536, 2560], P('req', 'tp')
The draws below stay inside these ranges and needn't reach their ends.
Inputs may be any that keep to these rules, and one draw needn't show every extreme that they name: `page_table`: the pages of the 4 requests of the d-th block of 4 rows are the d-th block of 64 pages of the pool, each named once. `cache_lengths`: some request holds 1024 positions. parents[r, 0] = -1, and 0 <= parents[r, i] < i for i >= 1. `routes`: A token's 6 experts differ. In each aligned block of 192 rows no expert is named by more than 91 rows, and in some block one expert is named by exactly 91.
All inputs are finite; a program needn't handle non-finite values.
Results may differ from the reference program's by a relative error of at most 0.02.
Values may be sent and summed in bfloat16 or wider, within the bound.
No kernel may reach another device: no remote copies, remote signals or barrier semaphores. Data moves between devices by JAX's collectives and lax.ppermute only.
A program may use at most 128 MiB of HBM per device.

```python
import math
import jax
import jax.numpy as jnp
import numpy as np
from jax import lax

D = 2560
QH = 20
KVH = 4
HD = 128
FFE = 1536
TOPK = 6
SFF = 1536
TREE = 48
PAGE = 64
REQ_DEV = 4
MAXP = 16
EXPERTS = 16
CTX = 1024
PAGES_DEV = 64
PAGES = 512
REQS = 32
TOKENS = 1536
CAP = 91
N_REQ = 8
N_TP = 4


def page_layout(key):
    groups = REQS // REQ_DEV
    subkeys = jax.random.split(jax.random.fold_in(key, 11), groups)
    orders = jax.vmap(lambda subkey: jax.random.permutation(subkey, PAGES_DEV))(subkeys)
    offset = (jnp.arange(groups, dtype=jnp.int32) * PAGES_DEV)[:, None]
    return (orders.astype(jnp.int32) + offset).reshape(REQS, MAXP)


def draw_page_table(key, part):
    return page_layout(key)


def draw_cache_lengths(key, part):
    first_draw = jax.random.randint(jax.random.fold_in(key, 31), (REQS,), 0, CTX - 1)
    second_draw = jax.random.randint(jax.random.fold_in(key, 32), (REQS,), 0, CTX - 1)
    lengths = 2 + jnp.minimum(first_draw, second_draw)
    position = jax.random.randint(jax.random.fold_in(key, 33), (), 0, REQS)
    return lengths.at[position].set(CTX).astype(jnp.int32)


def draw_parents(key, part):
    position = jnp.arange(TREE, dtype=jnp.int32)
    picks = jax.random.randint(jax.random.fold_in(key, 41), (REQS, TREE), 0, jnp.maximum(position, 1)[None, :])
    return jnp.where(position[None, :] == 0, -1, picks).astype(jnp.int32)


def draw_queries(key, part):
    values = jnp.clip(jax.random.normal(jax.random.fold_in(key, 51), (REQS, TREE, QH, HD), jnp.float32), -5.0, 5.0)
    return values.reshape(TOKENS, QH * HD).astype(jnp.bfloat16)


def draw_key_pages(key, part):
    values = jnp.clip(jax.random.normal(jax.random.fold_in(key, 61), (PAGES, PAGE, KVH * HD), jnp.float32), -5.0, 5.0)
    return values.astype(jnp.bfloat16)


def level_of(key, extent, cuts, low, high):
    def one(dim, blocks):
        steps = jax.random.uniform(jax.random.fold_in(jax.random.fold_in(key, 6), dim), (blocks,), jnp.float32, low / len(cuts), high / len(cuts))
        return jnp.repeat(jnp.exp(steps), extent[dim] // blocks).reshape((-1,) + (1,) * (len(extent) - dim - 1))

    factor_of = one(*cuts[0])
    for cut in cuts[1:]:
        factor_of = factor_of * one(*cut)
    return factor_of


def deal_out(rng, own, number, rows, amount, top, most, skew):
    ranking = jax.random.permutation(rng, amount)
    heavy_load, common = load_shares(amount, rows * top, most, skew, True), load_shares(amount, rows * top, most, skew, False)
    places = jnp.arange(amount)

    def named(tallies, turn):
        used = int((tallies > 0).sum())
        fixed = max(1, used // 4)
        shifted = fixed + (places - fixed + turn * (used - fixed)) % max(1, amount - fixed)
        return jnp.zeros((amount,), jnp.int32).at[ranking[jnp.where(places < fixed, places, shifted)]].set(jnp.asarray(tallies, jnp.int32))

    tallies = jnp.where(number % 4 == 0, named(heavy_load, number // 4), named(common, number - number // 4 - 1))
    mixed = jax.random.permutation(jax.random.fold_in(own, 3), amount)
    source_of, sink = mixed[0:amount // 2 * 2:2], mixed[1:amount // 2 * 2:2]
    room = jnp.minimum(tallies[source_of] - 1, most - tallies[sink]) // 2
    room = jnp.where((source_of == ranking[0]) | (sink == ranking[0]) | (tallies[sink] == 0), 0, jnp.maximum(room, 0))
    shifted = jax.random.randint(jax.random.fold_in(own, 4), (amount // 2,), 0, 1 << 20) % (room + 1)
    tallies = tallies.at[source_of].add(-shifted).at[sink].add(shifted)
    labels = jnp.searchsorted(jnp.cumsum(tallies), jnp.arange(rows * top), side="right").astype(jnp.int32)
    table = labels.reshape(top, rows).T
    table = table[jax.random.permutation(jax.random.fold_in(own, 1), rows)]
    turn = jax.random.randint(jax.random.fold_in(own, 2), (rows, 1), 0, top)
    return jnp.take_along_axis(table, (jnp.arange(top)[None, :] + turn) % top, axis=1)


def load_shares(number_of, total, bound, skew, full):
    loads = [(1 << 20) // math.isqrt(grade ** skew) + 1 for grade in range(1, number_of + 1)]
    largest = bound if full else min(bound, max(-(-total // number_of), total * loads[0] // sum(loads)))
    least = 1 if total - largest >= number_of - 1 else 0
    given, surplus = [largest] + [least] * (number_of - 1), total - largest - least * (number_of - 1)
    while surplus > 0:
        free = [i for i in range(1, number_of) if given[i] < largest] or [i for i in range(1, number_of) if given[i] < bound]
        whole, budget = sum([loads[i] for i in free]), surplus
        for i in free:
            addition = min(bound - given[i], max(1, budget * loads[i] // whole), surplus)
            given[i] = given[i] + addition
            surplus = surplus - addition
    return np.array(given)


def normal_values(rng, shape, width, bound, shards=(), kind=jnp.bfloat16):
    result = width * jax.random.normal(rng, shape, jnp.float32)
    if shards:
        result = result * level_of(rng, shape, shards, -0.22, 0.18)
    return jnp.clip(result, -bound, bound).astype(kind)


def setup_inputs(seed: int = 0) -> dict:
    key_of = jax.random.split(jax.random.key(seed), 18)
    queries = draw_queries(jax.random.fold_in(key_of[17], 71), 0)
    new_keys = normal_values(key_of[1], (TOKENS, KVH * HD), 1.0, 5.0, ((0, 8), (1, 4)))
    new_values = normal_values(key_of[2], (TOKENS, KVH * HD), 1.0, 5.0, ((0, 8), (1, 4)))
    key_pages = draw_key_pages(jax.random.fold_in(key_of[17], 71), 0)
    value_pages = normal_values(key_of[4], (PAGES, PAGE, KVH * HD), 1.0, 5.0, ((0, 8), (2, 4)))
    page_table = draw_page_table(jax.random.fold_in(key_of[17], 71), 0)
    cache_lengths = draw_cache_lengths(jax.random.fold_in(key_of[17], 71), 0)
    parents = draw_parents(jax.random.fold_in(key_of[17], 71), 0)
    residual = normal_values(key_of[8], (TOKENS, D), 1.0, 6.0, ((0, 8),))
    out_weight = normal_values(key_of[9], (QH * HD, D), (QH * HD) ** -0.5, 0.125, ((0, 4),))
    norm_gain = jnp.clip(1.0 + 0.18 * jax.random.normal(key_of[10], (D,), jnp.float32), 0.1, 1.9)
    router_weight = normal_values(key_of[11], (D, EXPERTS), D ** -0.5, 0.125, (), jnp.float32)
    routes_keys = jax.random.split(jax.random.fold_in(key_of[12], 1), TOKENS // (REQ_DEV * TREE))
    routes_turns = jax.random.permutation(jax.random.fold_in(key_of[12], 3), TOKENS // (REQ_DEV * TREE))
    routes = jax.vmap(lambda own, number: deal_out(jax.random.fold_in(key_of[12], 2), own, number, REQ_DEV * TREE, EXPERTS, TOPK, CAP, 2))(routes_keys, routes_turns).reshape((TOKENS, TOPK))
    expert_gate_up = normal_values(key_of[13], (EXPERTS, D, 2, FFE), D ** -0.5, 0.125, ((0, 8), (3, 4)))
    expert_down = normal_values(key_of[14], (EXPERTS, FFE, D), FFE ** -0.5, 0.15625, ((0, 8), (1, 4)))
    shared_gate_up = normal_values(key_of[15], (D, 2, SFF), D ** -0.5, 0.125, ((2, 4),))
    shared_down = normal_values(key_of[16], (SFF, D), SFF ** -0.5, 0.15625, ((0, 4),))
    return {"queries": queries, "new_keys": new_keys, "new_values": new_values, "key_pages": key_pages, "value_pages": value_pages, "page_table": page_table, "cache_lengths": cache_lengths, "parents": parents, "residual": residual, "out_weight": out_weight, "norm_gain": norm_gain, "router_weight": router_weight, "routes": routes, "expert_gate_up": expert_gate_up, "expert_down": expert_down, "shared_gate_up": shared_gate_up, "shared_down": shared_down}


EPSILON = 1e-06
NEGATIVE = -1e+30

def rounded(values):
    return lax.optimization_barrier(values.astype(jnp.bfloat16)).astype(jnp.float32)

def ancestors(parents):
    tree_size = parents.shape[-1]
    position = jnp.arange(tree_size, dtype=jnp.int32)
    adjacency = (parents[..., :, None] == position[None, :]) | (position[:, None] == position[None, :])
    closure = adjacency.astype(jnp.float32)
    for doubling in range(max(1, (tree_size - 1).bit_length())):
        closure = jnp.minimum(jnp.einsum('...ij,...jk->...ik', closure, closure, precision=lax.Precision.HIGHEST), 1.0)
    return closure > 0.5

def tree_attention(queries, cache_keys, cache_values, new_keys, new_values, lengths, allowed):
    scaling = 1.0 / math.sqrt(queries.shape[-1])
    query_f = queries.astype(jnp.float32)
    cache_scores = jnp.einsum('rtkgd,rckd->rkgtc', query_f, cache_keys.astype(jnp.float32)) * scaling
    tree_scores = jnp.einsum('rtkgd,rskd->rkgts', query_f, new_keys.astype(jnp.float32)) * scaling
    live = jnp.arange(cache_keys.shape[1], dtype=jnp.int32)[None, :] < lengths[:, None]
    cache_scores = jnp.where(live[:, None, None, None, :], cache_scores, NEGATIVE)
    tree_scores = jnp.where(allowed[:, None, None, :, :], tree_scores, NEGATIVE)
    highest = jnp.maximum(lax.optimization_barrier(jnp.max(cache_scores, axis=-1)), lax.optimization_barrier(jnp.max(tree_scores, axis=-1)))[..., None]
    cache_exp = jnp.exp(cache_scores - highest)
    tree_exp = jnp.exp(tree_scores - highest)
    denominator = (lax.optimization_barrier(jnp.sum(cache_exp, axis=-1)) + lax.optimization_barrier(jnp.sum(tree_exp, axis=-1)))[..., None]
    cache_probs = rounded(cache_exp / denominator)
    tree_probs = rounded(tree_exp / denominator)
    mixed = jnp.einsum('rkgtc,rckd->rtkgd', cache_probs, cache_values.astype(jnp.float32))
    mixed = mixed + jnp.einsum('rkgts,rskd->rtkgd', tree_probs, new_values.astype(jnp.float32))
    return mixed.astype(jnp.bfloat16).reshape(queries.shape[0], queries.shape[1], -1)

def reference(queries, new_keys, new_values, key_pages, value_pages, page_table, cache_lengths, parents, residual, out_weight, norm_gain, router_weight, routes, expert_gate_up, expert_down, shared_gate_up, shared_down):
    head_ratio = QH // KVH
    allowed = ancestors(parents)

    def one_request(items):
        query_rows, key_rows, value_rows, pages, length, mask = items
        cache_keys = key_pages[pages].reshape(1, CTX, KVH, HD)
        cache_values = value_pages[pages].reshape(1, CTX, KVH, HD)
        mixed = tree_attention(query_rows.reshape(1, TREE, KVH, head_ratio, HD), cache_keys, cache_values, key_rows.reshape(1, TREE, KVH, HD), value_rows.reshape(1, TREE, KVH, HD), length[None], mask[None])
        return mixed[0]
    head_outputs = lax.map(one_request, (queries.reshape(REQS, TREE, QH * HD), new_keys.reshape(REQS, TREE, KVH * HD), new_values.reshape(REQS, TREE, KVH * HD), page_table, cache_lengths, allowed))
    head_outputs = head_outputs.reshape(TOKENS, QH * HD)
    attn_out = jnp.dot(head_outputs, out_weight, preferred_element_type=jnp.float32)
    hidden = rounded(residual.astype(jnp.float32) + attn_out)
    rstd = lax.rsqrt(lax.optimization_barrier(jnp.mean(hidden * hidden, axis=1, keepdims=True)) + EPSILON)
    normed = hidden * rstd * norm_gain
    logits = jnp.dot(normed, router_weight, precision=lax.Precision.HIGHEST)
    normed_bf = rounded(normed)
    chosen = jnp.take_along_axis(logits, routes, axis=1)
    gate_values = jax.nn.sigmoid(chosen)
    gate_values = gate_values / lax.optimization_barrier(jnp.sum(gate_values, axis=1, keepdims=True))
    flat_expert = routes.reshape(-1)
    flat_gate = gate_values.reshape(-1)
    slot_count = N_REQ * CAP
    group_width = FFE // N_TP

    def one_expert(combined, expert):
        selected = flat_expert == expert
        found = jnp.nonzero(selected, size=slot_count, fill_value=0)[0].astype(jnp.int32)
        valid = jnp.arange(slot_count, dtype=jnp.int32) < jnp.sum(selected.astype(jnp.int32))
        token = found // TOPK
        inputs_f = normed_bf[token]
        gate_up = jnp.einsum('md,dcf->mcf', inputs_f, expert_gate_up[expert].astype(jnp.float32))
        act = rounded(jax.nn.silu(gate_up[:, 0]) * gate_up[:, 1])
        down_groups = expert_down[expert].astype(jnp.float32).reshape(N_TP, group_width, D)
        partial_value = jnp.einsum('mgf,gfd->mgd', act.reshape(slot_count, N_TP, group_width), down_groups)
        expert_out = rounded(lax.optimization_barrier(jnp.sum(rounded(partial_value), axis=1)))
        weight = jnp.where(valid, flat_gate[found], 0.0)
        combined = combined.at[token].add(weight[:, None] * expert_out)
        return (combined, None)
    combined = lax.scan(one_expert, jnp.zeros((TOKENS, D), jnp.float32), jnp.arange(EXPERTS, dtype=jnp.int32))[0]
    shared_gu = jnp.einsum('td,dcf->tcf', normed_bf, shared_gate_up.astype(jnp.float32))
    shared_act = rounded(jax.nn.silu(shared_gu[:, 0]) * shared_gu[:, 1])
    shared_out = jnp.dot(shared_act, shared_down.astype(jnp.float32))
    return (hidden + shared_out + combined).astype(jnp.bfloat16)
```

```python
import math

import jax
import jax.numpy as jnp
from jax import lax
from jax.sharding import PartitionSpec as P

QH = 20
KVH = 4
HD = 128


EPSILON = 1e-06
NEGATIVE = -1e30


def rounded(values):
    return lax.optimization_barrier(values.astype(jnp.bfloat16)).astype(jnp.float32)


def ancestors(parents):
    tree_size = parents.shape[-1]
    position = jnp.arange(tree_size, dtype=jnp.int32)
    adjacency = (parents[..., :, None] == position[None, :]) | (
        position[:, None] == position[None, :]
    )
    closure = adjacency.astype(jnp.float32)
    for doubling in range(max(1, (tree_size - 1).bit_length())):
        closure = jnp.minimum(
            jnp.einsum("...ij,...jk->...ik", closure, closure, precision=lax.Precision.HIGHEST), 1.0
        )
    return closure > 0.5


def tree_attention(queries, cache_keys, cache_values, new_keys, new_values, lengths, allowed):
    scaling = 1.0 / math.sqrt(queries.shape[-1])
    cache_scores = (
        jnp.einsum("rtkgd,rckd->rkgtc", queries, cache_keys, preferred_element_type=jnp.float32)
        * scaling
    )
    tree_scores = (
        jnp.einsum("rtkgd,rskd->rkgts", queries, new_keys, preferred_element_type=jnp.float32)
        * scaling
    )
    live = jnp.arange(cache_keys.shape[1], dtype=jnp.int32)[None, :] < lengths[:, None]
    cache_scores = jnp.where(live[:, None, None, None, :], cache_scores, NEGATIVE)
    tree_scores = jnp.where(allowed[:, None, None, :, :], tree_scores, NEGATIVE)
    highest = jnp.maximum(jnp.max(cache_scores, axis=-1), jnp.max(tree_scores, axis=-1))[..., None]
    cache_exp = jnp.exp(cache_scores - highest)
    tree_exp = jnp.exp(tree_scores - highest)
    denominator = (jnp.sum(cache_exp, axis=-1) + jnp.sum(tree_exp, axis=-1))[..., None]
    cache_probs = (cache_exp / denominator).astype(jnp.bfloat16)
    tree_probs = (tree_exp / denominator).astype(jnp.bfloat16)
    mixed = jnp.einsum(
        "rkgtc,rckd->rtkgd", cache_probs, cache_values, preferred_element_type=jnp.float32
    )
    mixed = mixed + jnp.einsum(
        "rkgts,rskd->rtkgd", tree_probs, new_values, preferred_element_type=jnp.float32
    )
    return mixed.astype(jnp.bfloat16).reshape(queries.shape[0], queries.shape[1], -1)


def shards(
    queries,
    new_keys,
    new_values,
    key_pages,
    value_pages,
    page_table,
    cache_lengths,
    parents,
    residual,
    out_weight,
    norm_gain,
    router_weight,
    routes,
    expert_gate_up,
    expert_down,
    shared_gate_up,
    shared_down,
):
    groups = lax.axis_size("req")
    tp_count = lax.axis_size("tp")
    requests = parents.shape[0]
    tree_size = parents.shape[1]
    row_count = requests * tree_size
    kv_local = new_keys.shape[1] // HD
    head_ratio = QH // KVH
    model_width = residual.shape[1]
    part_width = model_width // tp_count
    pages_dev = key_pages.shape[0]
    local_pages = page_table - lax.axis_index("req") * pages_dev
    cache_keys = key_pages[local_pages].reshape(requests, -1, kv_local, HD)
    cache_values = value_pages[local_pages].reshape(requests, -1, kv_local, HD)
    head_outputs = tree_attention(
        queries.reshape(requests, tree_size, kv_local, head_ratio, HD),
        cache_keys,
        cache_values,
        new_keys.reshape(requests, tree_size, kv_local, HD),
        new_values.reshape(requests, tree_size, kv_local, HD),
        cache_lengths,
        ancestors(parents),
    )
    attn_terms = jnp.dot(
        head_outputs.reshape(row_count, -1), out_weight, preferred_element_type=jnp.float32
    )
    column = lax.axis_index("tp") * part_width
    experts_local = expert_gate_up.shape[0]
    top_count = routes.shape[1]
    expert_count = experts_local * groups
    capacity = max(10 * requests, row_count * top_count * 5 // (4 * expert_count) + 1)
    capacity = -(-capacity // 16) * 16
    slot_count = expert_count * capacity

    flat_expert = routes.reshape(-1)
    expert_ids = jnp.arange(expert_count, dtype=jnp.int32)
    onehot = (flat_expert[:, None] == expert_ids[None, :]).astype(jnp.int32)
    earlier = jnp.cumsum(onehot, axis=0) - onehot
    rank = jnp.sum(earlier * onehot, axis=1)
    slot = (flat_expert * capacity + rank).reshape(row_count, top_count)
    slot_ids = jnp.arange(slot_count, dtype=jnp.int32)
    hit = slot[:, :, None] == slot_ids[None, None, :]

    attn_out = lax.psum(attn_terms.astype(jnp.bfloat16), "tp").astype(jnp.float32)
    hidden = rounded(residual.astype(jnp.float32) + attn_out)
    rstd = lax.rsqrt(jnp.mean(hidden * hidden, axis=1, keepdims=True) + EPSILON)
    normed = hidden * rstd * norm_gain
    logits = jnp.dot(normed, router_weight, precision=lax.Precision.HIGHEST)
    normed_bf = normed.astype(jnp.bfloat16)
    hidden_part = lax.dynamic_slice_in_dim(hidden, column, part_width, 1)

    dispatch = jnp.any(hit, axis=1).astype(jnp.bfloat16)
    outbox = jnp.einsum(
        "ts,td->sd", dispatch, normed_bf, preferred_element_type=jnp.float32
    ).astype(jnp.bfloat16)
    outbox = outbox.reshape(groups, experts_local * capacity, model_width)
    arrived = lax.all_to_all(outbox, "req", split_axis=0, concat_axis=0, tiled=True)
    arrived = arrived.reshape(groups, experts_local, capacity, model_width)
    results = []
    for expert in range(experts_local):
        rows = arrived[:, expert].reshape(groups * capacity, model_width)
        gate_up = jnp.einsum(
            "md,dcf->mcf", rows, expert_gate_up[expert], preferred_element_type=jnp.float32
        )
        act = (jax.nn.silu(gate_up[:, 0]) * gate_up[:, 1]).astype(jnp.bfloat16)
        partial_value = jnp.dot(act, expert_down[expert], preferred_element_type=jnp.float32)
        results.append(partial_value.astype(jnp.bfloat16).reshape(groups, capacity, model_width))
    outputs = jnp.stack(results, axis=1).reshape(groups, experts_local * capacity, model_width)
    returned = lax.all_to_all(outputs, "req", split_axis=0, concat_axis=0, tiled=True)
    returned = returned.reshape(slot_count, model_width)

    chosen = jnp.sum(
        jnp.where(routes[:, :, None] == expert_ids[None, None, :], logits[:, None, :], 0.0), axis=-1
    )
    gate_values = jax.nn.sigmoid(chosen)
    gate_values = gate_values / jnp.sum(gate_values, axis=1, keepdims=True)
    weights = jnp.sum(jnp.where(hit, gate_values[:, :, None], 0.0), axis=1)
    weights_hi = weights.astype(jnp.bfloat16)
    weights_lo = (weights - weights_hi.astype(jnp.float32)).astype(jnp.bfloat16)
    routed = jnp.dot(weights_hi, returned, preferred_element_type=jnp.float32) + jnp.dot(
        weights_lo, returned, preferred_element_type=jnp.float32
    )

    shared_gu = jnp.einsum(
        "td,dcf->tcf", normed_bf, shared_gate_up, preferred_element_type=jnp.float32
    )
    shared_act = (jax.nn.silu(shared_gu[:, 0]) * shared_gu[:, 1]).astype(jnp.bfloat16)
    shared_terms = jnp.dot(shared_act, shared_down, preferred_element_type=jnp.float32)
    summed = lax.psum_scatter(
        (shared_terms + routed).astype(jnp.bfloat16), "tp", scatter_dimension=1, tiled=True
    ).astype(jnp.float32)
    return (hidden_part + summed).astype(jnp.bfloat16)


def solution(mesh):
    in_specs = (
        P("req", "tp"),
        P("req", "tp"),
        P("req", "tp"),
        P("req", None, "tp"),
        P("req", None, "tp"),
        P("req", None),
        P("req"),
        P("req", None),
        P("req", None),
        P("tp", None),
        P(),
        P(),
        P("req", None),
        P("req", None, None, "tp"),
        P("req", "tp", None),
        P(None, None, "tp"),
        P("tp", None),
    )
    out_specs = P("req", "tp")
    return jax.shard_map(shards, mesh=mesh, in_specs=in_specs, out_specs=out_specs, check_vma=False)
```

```python
import math

import jax
import jax.numpy as jnp
from jax import lax
from jax.sharding import PartitionSpec as P

QH = 20
KVH = 4
HD = 128


EPSILON = 1e-06
NEGATIVE = -1e30


def rounded(values):
    return lax.optimization_barrier(values.astype(jnp.bfloat16)).astype(jnp.float32)


def ancestors(parents):
    tree_size = parents.shape[-1]
    position = jnp.arange(tree_size, dtype=jnp.int32)
    adjacency = (parents[..., :, None] == position[None, :]) | (
        position[:, None] == position[None, :]
    )
    closure = adjacency.astype(jnp.float32)
    for doubling in range(max(1, (tree_size - 1).bit_length())):
        closure = jnp.minimum(
            jnp.einsum("...ij,...jk->...ik", closure, closure, precision=lax.Precision.HIGHEST), 1.0
        )
    return closure > 0.5


def tree_attention(queries, cache_keys, cache_values, new_keys, new_values, lengths, allowed):
    scaling = 1.0 / math.sqrt(queries.shape[-1])
    cache_scores = (
        jnp.einsum("rtkgd,rckd->rkgtc", queries, cache_keys, preferred_element_type=jnp.float32)
        * scaling
    )
    tree_scores = (
        jnp.einsum("rtkgd,rskd->rkgts", queries, new_keys, preferred_element_type=jnp.float32)
        * scaling
    )
    live = jnp.arange(cache_keys.shape[1], dtype=jnp.int32)[None, :] < lengths[:, None]
    cache_scores = jnp.where(live[:, None, None, None, :], cache_scores, NEGATIVE)
    tree_scores = jnp.where(allowed[:, None, None, :, :], tree_scores, NEGATIVE)
    highest = jnp.maximum(jnp.max(cache_scores, axis=-1), jnp.max(tree_scores, axis=-1))[..., None]
    cache_exp = jnp.exp(cache_scores - highest)
    tree_exp = jnp.exp(tree_scores - highest)
    denominator = (jnp.sum(cache_exp, axis=-1) + jnp.sum(tree_exp, axis=-1))[..., None]
    cache_probs = (cache_exp / denominator).astype(jnp.bfloat16)
    tree_probs = (tree_exp / denominator).astype(jnp.bfloat16)
    mixed = jnp.einsum(
        "rkgtc,rckd->rtkgd", cache_probs, cache_values, preferred_element_type=jnp.float32
    )
    mixed = mixed + jnp.einsum(
        "rkgts,rskd->rtkgd", tree_probs, new_values, preferred_element_type=jnp.float32
    )
    return mixed.astype(jnp.bfloat16).reshape(queries.shape[0], queries.shape[1], -1)


def shards(
    queries,
    new_keys,
    new_values,
    key_pages,
    value_pages,
    page_table,
    cache_lengths,
    parents,
    residual,
    out_weight,
    norm_gain,
    router_weight,
    routes,
    expert_gate_up,
    expert_down,
    shared_gate_up,
    shared_down,
):
    groups = lax.axis_size("req")
    tp_count = lax.axis_size("tp")
    requests = parents.shape[0]
    tree_size = parents.shape[1]
    row_count = requests * tree_size
    kv_local = new_keys.shape[1] // HD
    head_ratio = QH // KVH
    model_width = residual.shape[1]
    part_width = model_width // tp_count
    pages_dev = key_pages.shape[0]
    local_pages = page_table - lax.axis_index("req") * pages_dev
    cache_keys = key_pages[local_pages].reshape(requests, -1, kv_local, HD)
    cache_values = value_pages[local_pages].reshape(requests, -1, kv_local, HD)
    head_outputs = tree_attention(
        queries.reshape(requests, tree_size, kv_local, head_ratio, HD),
        cache_keys,
        cache_values,
        new_keys.reshape(requests, tree_size, kv_local, HD),
        new_values.reshape(requests, tree_size, kv_local, HD),
        cache_lengths,
        ancestors(parents),
    )
    attn_terms = jnp.dot(
        head_outputs.reshape(row_count, -1), out_weight, preferred_element_type=jnp.float32
    )
    column = lax.axis_index("tp") * part_width
    experts_local = expert_gate_up.shape[0]
    top_count = routes.shape[1]
    expert_count = experts_local * groups
    capacity = max(10 * requests, row_count * top_count * 5 // (4 * expert_count) + 1)
    capacity = -(-capacity // 16) * 16
    slot_count = expert_count * capacity

    flat_expert = routes.reshape(-1)
    expert_ids = jnp.arange(expert_count, dtype=jnp.int32)
    onehot = (flat_expert[:, None] == expert_ids[None, :]).astype(jnp.int32)
    earlier = jnp.cumsum(onehot, axis=0) - onehot
    rank = jnp.sum(earlier * onehot, axis=1)
    slot = (flat_expert * capacity + rank).reshape(row_count, top_count)
    slot_ids = jnp.arange(slot_count, dtype=jnp.int32)
    hit = slot[:, :, None] == slot_ids[None, None, :]

    attn_blocks = attn_terms.astype(jnp.bfloat16).reshape(row_count, tp_count, part_width)
    attn_blocks = lax.all_to_all(
        attn_blocks.transpose(1, 0, 2), "tp", split_axis=0, concat_axis=0, tiled=True
    )
    attn_part = jnp.sum(attn_blocks.astype(jnp.float32), axis=0)
    residual_part = lax.dynamic_slice_in_dim(residual, column, part_width, 1)
    hidden_part_bf = (residual_part.astype(jnp.float32) + attn_part).astype(jnp.bfloat16)
    hidden_bf = lax.all_gather(hidden_part_bf[None], "tp", axis=0, tiled=True)
    hidden = hidden_bf.transpose(1, 0, 2).reshape(row_count, model_width).astype(jnp.float32)
    rstd = lax.rsqrt(jnp.mean(hidden * hidden, axis=1, keepdims=True) + EPSILON)
    normed = hidden * rstd * norm_gain
    logits = jnp.dot(normed, router_weight, precision=lax.Precision.HIGHEST)
    normed_bf = normed.astype(jnp.bfloat16)
    hidden_part = hidden_part_bf.astype(jnp.float32)

    dispatch = jnp.any(hit, axis=1).astype(jnp.bfloat16)
    dispatch = dispatch.reshape(row_count, groups, experts_local, capacity)
    returns = []
    for expert in range(experts_local):
        outbox = jnp.einsum(
            "tgc,td->gcd", dispatch[:, :, expert], normed_bf, preferred_element_type=jnp.float32
        ).astype(jnp.bfloat16)
        arrived = lax.all_to_all(outbox, "req", split_axis=0, concat_axis=0, tiled=True)
        rows = arrived.reshape(groups * capacity, model_width)
        gate_up = jnp.einsum(
            "md,dcf->mcf", rows, expert_gate_up[expert], preferred_element_type=jnp.float32
        )
        act = (jax.nn.silu(gate_up[:, 0]) * gate_up[:, 1]).astype(jnp.bfloat16)
        partial_value = jnp.dot(act, expert_down[expert], preferred_element_type=jnp.float32)
        outputs = partial_value.astype(jnp.bfloat16).reshape(groups, capacity, model_width)
        returns.append(lax.all_to_all(outputs, "req", split_axis=0, concat_axis=0, tiled=True))

    chosen = jnp.sum(
        jnp.where(routes[:, :, None] == expert_ids[None, None, :], logits[:, None, :], 0.0), axis=-1
    )
    gate_values = jax.nn.sigmoid(chosen)
    gate_values = gate_values / jnp.sum(gate_values, axis=1, keepdims=True)
    weights = jnp.sum(jnp.where(hit, gate_values[:, :, None], 0.0), axis=1)
    weights = weights.reshape(row_count, groups, experts_local, capacity)
    weights_hi = weights.astype(jnp.bfloat16)
    weights_lo = (weights - weights_hi.astype(jnp.float32)).astype(jnp.bfloat16)
    routed = jnp.zeros((row_count, model_width), jnp.float32)
    for expert in range(experts_local):
        for split in (weights_hi, weights_lo):
            routed = routed + jnp.einsum(
                "tgc,gcd->td", split[:, :, expert], returns[expert],
                preferred_element_type=jnp.float32,
            )

    shared_gu = jnp.einsum(
        "td,dcf->tcf", normed_bf, shared_gate_up, preferred_element_type=jnp.float32
    )
    shared_act = (jax.nn.silu(shared_gu[:, 0]) * shared_gu[:, 1]).astype(jnp.bfloat16)
    shared_terms = jnp.dot(shared_act, shared_down, preferred_element_type=jnp.float32)
    total = (shared_terms + routed).astype(jnp.bfloat16).reshape(row_count, tp_count, part_width)
    total = lax.all_to_all(total.transpose(1, 0, 2), "tp", split_axis=0, concat_axis=0, tiled=True)
    summed = jnp.sum(total.astype(jnp.float32), axis=0)
    return (hidden_part + summed).astype(jnp.bfloat16)


def solution(mesh):
    in_specs = (
        P("req", "tp"),
        P("req", "tp"),
        P("req", "tp"),
        P("req", None, "tp"),
        P("req", None, "tp"),
        P("req", None),
        P("req"),
        P("req", None),
        P("req", None),
        P("tp", None),
        P(),
        P(),
        P("req", None),
        P("req", None, None, "tp"),
        P("req", "tp", None),
        P(None, None, "tp"),
        P("tp", None),
    )
    out_specs = P("req", "tp")
    return jax.shard_map(shards, mesh=mesh, in_specs=in_specs, out_specs=out_specs, check_vma=False)
```

```python
import math

import jax
import jax.numpy as jnp
from jax import lax
from jax.sharding import PartitionSpec as P

QH = 20
KVH = 4
HD = 128


EPSILON = 1e-06
NEGATIVE = -1e30


def rounded(values):
    return lax.optimization_barrier(values.astype(jnp.bfloat16)).astype(jnp.float32)


def ancestors(parents):
    tree_size = parents.shape[-1]
    position = jnp.arange(tree_size, dtype=jnp.int32)
    adjacency = (parents[..., :, None] == position[None, :]) | (
        position[:, None] == position[None, :]
    )
    closure = adjacency.astype(jnp.float32)
    for doubling in range(max(1, (tree_size - 1).bit_length())):
        closure = jnp.minimum(
            jnp.einsum("...ij,...jk->...ik", closure, closure, precision=lax.Precision.HIGHEST), 1.0
        )
    return closure > 0.5


def tree_attention(queries, cache_keys, cache_values, new_keys, new_values, lengths, allowed):
    scaling = 1.0 / math.sqrt(queries.shape[-1])
    cache_scores = (
        jnp.einsum("rtkgd,rckd->rkgtc", queries, cache_keys, preferred_element_type=jnp.float32)
        * scaling
    )
    tree_scores = (
        jnp.einsum("rtkgd,rskd->rkgts", queries, new_keys, preferred_element_type=jnp.float32)
        * scaling
    )
    live = jnp.arange(cache_keys.shape[1], dtype=jnp.int32)[None, :] < lengths[:, None]
    cache_scores = jnp.where(live[:, None, None, None, :], cache_scores, NEGATIVE)
    tree_scores = jnp.where(allowed[:, None, None, :, :], tree_scores, NEGATIVE)
    highest = jnp.maximum(jnp.max(cache_scores, axis=-1), jnp.max(tree_scores, axis=-1))[..., None]
    cache_exp = jnp.exp(cache_scores - highest)
    tree_exp = jnp.exp(tree_scores - highest)
    denominator = (jnp.sum(cache_exp, axis=-1) + jnp.sum(tree_exp, axis=-1))[..., None]
    cache_probs = (cache_exp / denominator).astype(jnp.bfloat16)
    tree_probs = (tree_exp / denominator).astype(jnp.bfloat16)
    mixed = jnp.einsum(
        "rkgtc,rckd->rtkgd", cache_probs, cache_values, preferred_element_type=jnp.float32
    )
    mixed = mixed + jnp.einsum(
        "rkgts,rskd->rtkgd", tree_probs, new_values, preferred_element_type=jnp.float32
    )
    return mixed.astype(jnp.bfloat16).reshape(queries.shape[0], queries.shape[1], -1)


def shards(
    queries,
    new_keys,
    new_values,
    key_pages,
    value_pages,
    page_table,
    cache_lengths,
    parents,
    residual,
    out_weight,
    norm_gain,
    router_weight,
    routes,
    expert_gate_up,
    expert_down,
    shared_gate_up,
    shared_down,
):
    groups = lax.axis_size("req")
    tp_count = lax.axis_size("tp")
    requests = parents.shape[0]
    tree_size = parents.shape[1]
    row_count = requests * tree_size
    kv_local = new_keys.shape[1] // HD
    head_ratio = QH // KVH
    model_width = residual.shape[1]
    part_width = model_width // tp_count
    pages_dev = key_pages.shape[0]
    local_pages = page_table - lax.axis_index("req") * pages_dev
    cache_keys = key_pages[local_pages].reshape(requests, -1, kv_local, HD)
    cache_values = value_pages[local_pages].reshape(requests, -1, kv_local, HD)
    head_outputs = tree_attention(
        queries.reshape(requests, tree_size, kv_local, head_ratio, HD),
        cache_keys,
        cache_values,
        new_keys.reshape(requests, tree_size, kv_local, HD),
        new_values.reshape(requests, tree_size, kv_local, HD),
        cache_lengths,
        ancestors(parents),
    )
    attn_terms = jnp.dot(
        head_outputs.reshape(row_count, -1), out_weight, preferred_element_type=jnp.float32
    )
    column = lax.axis_index("tp") * part_width
    experts_local = expert_gate_up.shape[0]
    top_count = routes.shape[1]
    expert_count = experts_local * groups
    capacity = max(10 * requests, row_count * top_count * 5 // (4 * expert_count) + 1)
    capacity = -(-capacity // 16) * 16
    slot_count = expert_count * capacity

    flat_expert = routes.reshape(-1)
    expert_ids = jnp.arange(expert_count, dtype=jnp.int32)
    onehot = (flat_expert[:, None] == expert_ids[None, :]).astype(jnp.int32)
    earlier = jnp.cumsum(onehot, axis=0) - onehot
    rank = jnp.sum(earlier * onehot, axis=1)
    slot = (flat_expert * capacity + rank).reshape(row_count, top_count)
    slot_ids = jnp.arange(slot_count, dtype=jnp.int32)
    hit = slot[:, :, None] == slot_ids[None, None, :]

    attn_blocks = attn_terms.astype(jnp.bfloat16).reshape(row_count, tp_count, part_width)
    attn_blocks = lax.all_to_all(
        attn_blocks.transpose(1, 0, 2), "tp", split_axis=0, concat_axis=0, tiled=True
    )
    attn_part = jnp.sum(attn_blocks.astype(jnp.float32), axis=0)
    residual_part = lax.dynamic_slice_in_dim(residual, column, part_width, 1)
    hidden_part_bf = (residual_part.astype(jnp.float32) + attn_part).astype(jnp.bfloat16)
    hidden_bf = lax.all_gather(hidden_part_bf[None], "tp", axis=0, tiled=True)
    hidden = hidden_bf.transpose(1, 0, 2).reshape(row_count, model_width).astype(jnp.float32)
    rstd = lax.rsqrt(jnp.mean(hidden * hidden, axis=1, keepdims=True) + EPSILON)
    normed = hidden * rstd * norm_gain
    logits = jnp.dot(normed, router_weight, precision=lax.Precision.HIGHEST)
    normed_bf = normed.astype(jnp.bfloat16)
    hidden_part = hidden_part_bf.astype(jnp.float32)

    near_width = part_width // 2
    far_width = part_width - near_width
    normed_blocks = normed_bf.reshape(row_count, tp_count, part_width)
    normed_near = normed_blocks[:, :, :near_width].reshape(row_count, tp_count * near_width)
    normed_far = lax.dynamic_slice_in_dim(normed_bf, column + near_width, far_width, 1)
    send_rows = jnp.concatenate([normed_near, normed_far], axis=1)
    dispatch = jnp.any(hit, axis=1).astype(jnp.bfloat16)
    dispatch = dispatch.reshape(row_count, groups, experts_local, capacity)
    returns = []
    for expert in range(experts_local):
        outbox = jnp.einsum(
            "tgc,tk->gck", dispatch[:, :, expert], send_rows, preferred_element_type=jnp.float32
        ).astype(jnp.bfloat16)
        arrived = lax.all_to_all(outbox, "req", split_axis=0, concat_axis=0, tiled=True)
        arrived = arrived.reshape(groups * capacity, -1)
        rows_near = arrived[:, : tp_count * near_width]
        rows_far = lax.all_gather(
            arrived[None, :, tp_count * near_width :], "tp", axis=0, tiled=True
        )
        weight_blocks = expert_gate_up[expert].reshape(tp_count, part_width, 2, -1)
        weight_near = weight_blocks[:, :near_width].reshape(tp_count * near_width, 2, -1)
        weight_far = weight_blocks[:, near_width:]
        gate_up = jnp.einsum(
            "mk,kcf->mcf", rows_near, weight_near, preferred_element_type=jnp.float32
        ) + jnp.einsum("zmk,zkcf->mcf", rows_far, weight_far, preferred_element_type=jnp.float32)
        act = (jax.nn.silu(gate_up[:, 0]) * gate_up[:, 1]).astype(jnp.bfloat16)
        partial_value = jnp.dot(act, expert_down[expert], preferred_element_type=jnp.float32)
        partial_blocks = partial_value.astype(jnp.bfloat16).reshape(-1, tp_count, part_width)
        back_near = partial_blocks[:, :, :near_width].reshape(-1, tp_count * near_width)
        far_parts = lax.all_to_all(
            partial_blocks[:, :, near_width:].transpose(1, 0, 2),
            "tp", split_axis=0, concat_axis=0, tiled=True,
        )
        back_far = jnp.sum(far_parts.astype(jnp.float32), axis=0).astype(jnp.bfloat16)
        outputs = jnp.concatenate([back_near, back_far], axis=1).reshape(groups, capacity, -1)
        returns.append(lax.all_to_all(outputs, "req", split_axis=0, concat_axis=0, tiled=True))

    chosen = jnp.sum(
        jnp.where(routes[:, :, None] == expert_ids[None, None, :], logits[:, None, :], 0.0), axis=-1
    )
    gate_values = jax.nn.sigmoid(chosen)
    gate_values = gate_values / jnp.sum(gate_values, axis=1, keepdims=True)
    weights = jnp.sum(jnp.where(hit, gate_values[:, :, None], 0.0), axis=1)
    weights = weights.reshape(row_count, groups, experts_local, capacity)
    weights_hi = weights.astype(jnp.bfloat16)
    weights_lo = (weights - weights_hi.astype(jnp.float32)).astype(jnp.bfloat16)
    routed = jnp.zeros((row_count, tp_count * near_width + far_width), jnp.float32)
    for expert in range(experts_local):
        for split in (weights_hi, weights_lo):
            routed = routed + jnp.einsum(
                "tgc,gck->tk", split[:, :, expert], returns[expert],
                preferred_element_type=jnp.float32,
            )
    routed_near = routed[:, : tp_count * near_width].reshape(row_count, tp_count, near_width)
    routed_far = routed[:, tp_count * near_width :]

    shared_gu = jnp.einsum(
        "td,dcf->tcf", normed_bf, shared_gate_up, preferred_element_type=jnp.float32
    )
    shared_act = (jax.nn.silu(shared_gu[:, 0]) * shared_gu[:, 1]).astype(jnp.bfloat16)
    shared_terms = jnp.dot(shared_act, shared_down, preferred_element_type=jnp.float32)
    shared_blocks = shared_terms.reshape(row_count, tp_count, part_width)
    total = jnp.concatenate(
        [shared_blocks[:, :, :near_width] + routed_near, shared_blocks[:, :, near_width:]], axis=2
    ).astype(jnp.bfloat16)
    total = lax.all_to_all(total.transpose(1, 0, 2), "tp", split_axis=0, concat_axis=0, tiled=True)
    summed = jnp.sum(total.astype(jnp.float32), axis=0)
    summed = summed + jnp.concatenate(
        [jnp.zeros((row_count, near_width), jnp.float32), routed_far], axis=1
    )
    return (hidden_part + summed).astype(jnp.bfloat16)


def solution(mesh):
    in_specs = (
        P("req", "tp"),
        P("req", "tp"),
        P("req", "tp"),
        P("req", None, "tp"),
        P("req", None, "tp"),
        P("req", None),
        P("req"),
        P("req", None),
        P("req", None),
        P("tp", None),
        P(),
        P(),
        P("req", None),
        P("req", None, None, "tp"),
        P("req", "tp", None),
        P(None, None, "tp"),
        P("tp", None),
    )
    out_specs = P("req", "tp")
    return jax.shard_map(shards, mesh=mesh, in_specs=in_specs, out_specs=out_specs, check_vma=False)
```

```python
import math

import jax
import jax.numpy as jnp
from jax import lax
from jax.sharding import PartitionSpec as P

QH = 20
KVH = 4
HD = 128


EPSILON = 1e-06
NEGATIVE = -1e30


def rounded(values):
    return lax.optimization_barrier(values.astype(jnp.bfloat16)).astype(jnp.float32)


def ancestors(parents):
    tree_size = parents.shape[-1]
    position = jnp.arange(tree_size, dtype=jnp.int32)
    adjacency = (parents[..., :, None] == position[None, :]) | (
        position[:, None] == position[None, :]
    )
    closure = adjacency.astype(jnp.float32)
    for doubling in range(max(1, (tree_size - 1).bit_length())):
        closure = jnp.minimum(
            jnp.einsum("...ij,...jk->...ik", closure, closure, precision=lax.Precision.HIGHEST), 1.0
        )
    return closure > 0.5


def tree_attention(queries, cache_keys, cache_values, new_keys, new_values, lengths, allowed):
    scaling = 1.0 / math.sqrt(queries.shape[-1])
    cache_scores = (
        jnp.einsum("rtkgd,rckd->rkgtc", queries, cache_keys, preferred_element_type=jnp.float32)
        * scaling
    )
    tree_scores = (
        jnp.einsum("rtkgd,rskd->rkgts", queries, new_keys, preferred_element_type=jnp.float32)
        * scaling
    )
    live = jnp.arange(cache_keys.shape[1], dtype=jnp.int32)[None, :] < lengths[:, None]
    cache_scores = jnp.where(live[:, None, None, None, :], cache_scores, NEGATIVE)
    tree_scores = jnp.where(allowed[:, None, None, :, :], tree_scores, NEGATIVE)
    highest = jnp.maximum(jnp.max(cache_scores, axis=-1), jnp.max(tree_scores, axis=-1))[..., None]
    cache_exp = jnp.exp(cache_scores - highest)
    tree_exp = jnp.exp(tree_scores - highest)
    denominator = (jnp.sum(cache_exp, axis=-1) + jnp.sum(tree_exp, axis=-1))[..., None]
    cache_probs = (cache_exp / denominator).astype(jnp.bfloat16)
    tree_probs = (tree_exp / denominator).astype(jnp.bfloat16)
    mixed = jnp.einsum(
        "rkgtc,rckd->rtkgd", cache_probs, cache_values, preferred_element_type=jnp.float32
    )
    mixed = mixed + jnp.einsum(
        "rkgts,rskd->rtkgd", tree_probs, new_values, preferred_element_type=jnp.float32
    )
    return mixed.astype(jnp.bfloat16).reshape(queries.shape[0], queries.shape[1], -1)


def shards(
    queries,
    new_keys,
    new_values,
    key_pages,
    value_pages,
    page_table,
    cache_lengths,
    parents,
    residual,
    out_weight,
    norm_gain,
    router_weight,
    routes,
    expert_gate_up,
    expert_down,
    shared_gate_up,
    shared_down,
):
    groups = lax.axis_size("req")
    tp_count = lax.axis_size("tp")
    requests = parents.shape[0]
    tree_size = parents.shape[1]
    row_count = requests * tree_size
    kv_local = new_keys.shape[1] // HD
    head_ratio = QH // KVH
    model_width = residual.shape[1]
    part_width = model_width // tp_count
    pages_dev = key_pages.shape[0]
    local_pages = page_table - lax.axis_index("req") * pages_dev
    cache_keys = key_pages[local_pages].reshape(requests, -1, kv_local, HD)
    cache_values = value_pages[local_pages].reshape(requests, -1, kv_local, HD)
    head_outputs = tree_attention(
        queries.reshape(requests, tree_size, kv_local, head_ratio, HD),
        cache_keys,
        cache_values,
        new_keys.reshape(requests, tree_size, kv_local, HD),
        new_values.reshape(requests, tree_size, kv_local, HD),
        cache_lengths,
        ancestors(parents),
    )
    attn_terms = jnp.dot(
        head_outputs.reshape(row_count, -1), out_weight, preferred_element_type=jnp.float32
    )
    column = lax.axis_index("tp") * part_width
    experts_local = expert_gate_up.shape[0]
    top_count = routes.shape[1]
    expert_count = experts_local * groups
    capacity = max(10 * requests, row_count * top_count * 5 // (4 * expert_count) + 1)
    capacity = -(-capacity // 16) * 16
    slot_count = expert_count * capacity

    flat_expert = routes.reshape(-1)
    expert_ids = jnp.arange(expert_count, dtype=jnp.int32)
    onehot = (flat_expert[:, None] == expert_ids[None, :]).astype(jnp.int32)
    earlier = jnp.cumsum(onehot, axis=0) - onehot
    rank = jnp.sum(earlier * onehot, axis=1)
    slot = (flat_expert * capacity + rank).reshape(row_count, top_count)
    slot_ids = jnp.arange(slot_count, dtype=jnp.int32)
    hit = slot[:, :, None] == slot_ids[None, None, :]

    attn_blocks = attn_terms.astype(jnp.bfloat16).reshape(row_count, tp_count, part_width)
    attn_blocks = lax.all_to_all(
        attn_blocks.transpose(1, 0, 2), "tp", split_axis=0, concat_axis=0, tiled=True
    )
    attn_part = jnp.sum(attn_blocks.astype(jnp.float32), axis=0)
    residual_part = lax.dynamic_slice_in_dim(residual, column, part_width, 1)
    hidden_part_bf = (residual_part.astype(jnp.float32) + attn_part).astype(jnp.bfloat16)
    hidden_bf = lax.all_gather(hidden_part_bf[None], "tp", axis=0, tiled=True)
    hidden = hidden_bf.transpose(1, 0, 2).reshape(row_count, model_width).astype(jnp.float32)
    rstd = lax.rsqrt(jnp.mean(hidden * hidden, axis=1, keepdims=True) + EPSILON)
    normed = hidden * rstd * norm_gain
    logits = jnp.dot(normed, router_weight, precision=lax.Precision.HIGHEST)
    normed_bf = normed.astype(jnp.bfloat16)
    hidden_part = hidden_part_bf.astype(jnp.float32)

    dispatch = jnp.any(hit, axis=1).astype(jnp.bfloat16)
    dispatch = dispatch.reshape(row_count, groups, experts_local * capacity)
    outbox = jnp.einsum(
        "tgc,td->gcd", dispatch, normed_bf, preferred_element_type=jnp.float32
    ).astype(jnp.bfloat16)
    arrived = lax.all_to_all(outbox, "req", split_axis=0, concat_axis=0, tiled=True)
    arrived = arrived.reshape(groups, experts_local, capacity, model_width)
    gate_up = jnp.einsum(
        "gecd,edkf->egckf", arrived, expert_gate_up, preferred_element_type=jnp.float32
    )
    act = (jax.nn.silu(gate_up[:, :, :, 0]) * gate_up[:, :, :, 1]).astype(jnp.bfloat16)
    partial_value = jnp.einsum(
        "egcf,efd->gecd", act, expert_down, preferred_element_type=jnp.float32
    ).astype(jnp.bfloat16)
    outputs = partial_value.reshape(groups, experts_local * capacity, model_width)
    returned = lax.all_to_all(outputs, "req", split_axis=0, concat_axis=0, tiled=True)

    chosen = jnp.sum(
        jnp.where(routes[:, :, None] == expert_ids[None, None, :], logits[:, None, :], 0.0), axis=-1
    )
    gate_values = jax.nn.sigmoid(chosen)
    gate_values = gate_values / jnp.sum(gate_values, axis=1, keepdims=True)
    weights = jnp.sum(jnp.where(hit, gate_values[:, :, None], 0.0), axis=1)
    weights = weights.reshape(row_count, groups, experts_local * capacity)
    weights_hi = weights.astype(jnp.bfloat16)
    weights_lo = (weights - weights_hi.astype(jnp.float32)).astype(jnp.bfloat16)
    routed = jnp.einsum(
        "tgc,gcd->td", weights_hi, returned, preferred_element_type=jnp.float32
    ) + jnp.einsum("tgc,gcd->td", weights_lo, returned, preferred_element_type=jnp.float32)

    shared_gu = jnp.einsum(
        "td,dcf->tcf", normed_bf, shared_gate_up, preferred_element_type=jnp.float32
    )
    shared_act = (jax.nn.silu(shared_gu[:, 0]) * shared_gu[:, 1]).astype(jnp.bfloat16)
    shared_terms = jnp.dot(shared_act, shared_down, preferred_element_type=jnp.float32)
    total = (shared_terms + routed).astype(jnp.bfloat16).reshape(row_count, tp_count, part_width)
    total = lax.all_to_all(total.transpose(1, 0, 2), "tp", split_axis=0, concat_axis=0, tiled=True)
    summed = jnp.sum(total.astype(jnp.float32), axis=0)
    return (hidden_part + summed).astype(jnp.bfloat16)


def solution(mesh):
    in_specs = (
        P("req", "tp"),
        P("req", "tp"),
        P("req", "tp"),
        P("req", None, "tp"),
        P("req", None, "tp"),
        P("req", None),
        P("req"),
        P("req", None),
        P("req", None),
        P("tp", None),
        P(),
        P(),
        P("req", None),
        P("req", None, None, "tp"),
        P("req", "tp", None),
        P(None, None, "tp"),
        P("tp", None),
    )
    out_specs = P("req", "tp")
    return jax.shard_map(shards, mesh=mesh, in_specs=in_specs, out_specs=out_specs, check_vma=False)
```

```python
import math

import jax
import jax.numpy as jnp
from jax import lax
from jax.sharding import PartitionSpec as P

QH = 20
KVH = 4
HD = 128


EPSILON = 1e-06
NEGATIVE = -1e30


def rounded(values):
    return lax.optimization_barrier(values.astype(jnp.bfloat16)).astype(jnp.float32)


def ancestors(parents):
    tree_size = parents.shape[-1]
    position = jnp.arange(tree_size, dtype=jnp.int32)
    adjacency = (parents[..., :, None] == position[None, :]) | (
        position[:, None] == position[None, :]
    )
    closure = adjacency.astype(jnp.float32)
    for doubling in range(max(1, (tree_size - 1).bit_length())):
        closure = jnp.minimum(
            jnp.einsum("...ij,...jk->...ik", closure, closure, precision=lax.Precision.HIGHEST), 1.0
        )
    return closure > 0.5


def tree_attention(queries, cache_keys, cache_values, new_keys, new_values, lengths, allowed):
    scaling = 1.0 / math.sqrt(queries.shape[-1])
    cache_scores = (
        jnp.einsum("rtkgd,rckd->rkgtc", queries, cache_keys, preferred_element_type=jnp.float32)
        * scaling
    )
    tree_scores = (
        jnp.einsum("rtkgd,rskd->rkgts", queries, new_keys, preferred_element_type=jnp.float32)
        * scaling
    )
    live = jnp.arange(cache_keys.shape[1], dtype=jnp.int32)[None, :] < lengths[:, None]
    cache_scores = jnp.where(live[:, None, None, None, :], cache_scores, NEGATIVE)
    tree_scores = jnp.where(allowed[:, None, None, :, :], tree_scores, NEGATIVE)
    highest = jnp.maximum(jnp.max(cache_scores, axis=-1), jnp.max(tree_scores, axis=-1))[..., None]
    cache_exp = jnp.exp(cache_scores - highest)
    tree_exp = jnp.exp(tree_scores - highest)
    denominator = (jnp.sum(cache_exp, axis=-1) + jnp.sum(tree_exp, axis=-1))[..., None]
    cache_probs = (cache_exp / denominator).astype(jnp.bfloat16)
    tree_probs = (tree_exp / denominator).astype(jnp.bfloat16)
    mixed = jnp.einsum(
        "rkgtc,rckd->rtkgd", cache_probs, cache_values, preferred_element_type=jnp.float32
    )
    mixed = mixed + jnp.einsum(
        "rkgts,rskd->rtkgd", tree_probs, new_values, preferred_element_type=jnp.float32
    )
    return mixed.astype(jnp.bfloat16).reshape(queries.shape[0], queries.shape[1], -1)


def shards(
    queries,
    new_keys,
    new_values,
    key_pages,
    value_pages,
    page_table,
    cache_lengths,
    parents,
    residual,
    out_weight,
    norm_gain,
    router_weight,
    routes,
    expert_gate_up,
    expert_down,
    shared_gate_up,
    shared_down,
):
    groups = lax.axis_size("req")
    tp_count = lax.axis_size("tp")
    requests = parents.shape[0]
    tree_size = parents.shape[1]
    row_count = requests * tree_size
    kv_local = new_keys.shape[1] // HD
    head_ratio = QH // KVH
    model_width = residual.shape[1]
    part_width = model_width // tp_count
    pages_dev = key_pages.shape[0]
    local_pages = page_table - lax.axis_index("req") * pages_dev
    cache_keys = key_pages[local_pages].reshape(requests, -1, kv_local, HD)
    cache_values = value_pages[local_pages].reshape(requests, -1, kv_local, HD)
    head_outputs = tree_attention(
        queries.reshape(requests, tree_size, kv_local, head_ratio, HD),
        cache_keys,
        cache_values,
        new_keys.reshape(requests, tree_size, kv_local, HD),
        new_values.reshape(requests, tree_size, kv_local, HD),
        cache_lengths,
        ancestors(parents),
    )
    attn_terms = jnp.dot(
        head_outputs.reshape(row_count, -1), out_weight, preferred_element_type=jnp.float32
    )
    column = lax.axis_index("tp") * part_width
    experts_local = expert_gate_up.shape[0]
    top_count = routes.shape[1]
    expert_count = experts_local * groups
    capacity = max(10 * requests, row_count * top_count * 5 // (4 * expert_count) + 1)
    capacity = -(-capacity // 16) * 16
    slot_count = expert_count * capacity

    flat_expert = routes.reshape(-1)
    expert_ids = jnp.arange(expert_count, dtype=jnp.int32)
    onehot = (flat_expert[:, None] == expert_ids[None, :]).astype(jnp.int32)
    earlier = jnp.cumsum(onehot, axis=0) - onehot
    rank = jnp.sum(earlier * onehot, axis=1)
    slot = (flat_expert * capacity + rank).reshape(row_count, top_count)
    slot_ids = jnp.arange(slot_count, dtype=jnp.int32)
    hit = slot[:, :, None] == slot_ids[None, None, :]

    attn_blocks = attn_terms.astype(jnp.bfloat16).reshape(row_count, tp_count, part_width)
    attn_blocks = lax.all_to_all(
        attn_blocks.transpose(1, 0, 2), "tp", split_axis=0, concat_axis=0, tiled=True
    )
    attn_part = jnp.sum(attn_blocks.astype(jnp.float32), axis=0)
    residual_part = lax.dynamic_slice_in_dim(residual, column, part_width, 1)
    hidden_part_bf = (residual_part.astype(jnp.float32) + attn_part).astype(jnp.bfloat16)
    hidden_bf = lax.all_gather(hidden_part_bf[None], "tp", axis=0, tiled=True)
    hidden = hidden_bf.transpose(1, 0, 2).reshape(row_count, model_width).astype(jnp.float32)
    rstd = lax.rsqrt(jnp.mean(hidden * hidden, axis=1, keepdims=True) + EPSILON)
    normed = hidden * rstd * norm_gain
    logits = jnp.dot(normed, router_weight, precision=lax.Precision.HIGHEST)
    normed_bf = normed.astype(jnp.bfloat16)
    hidden_part = hidden_part_bf.astype(jnp.float32)

    dispatch = jnp.any(hit, axis=1).astype(jnp.bfloat16)
    dispatch = dispatch.reshape(row_count, groups, experts_local, capacity)
    returns = []
    for expert in range(experts_local):
        outbox = jnp.einsum(
            "tgc,td->gcd", dispatch[:, :, expert], normed_bf, preferred_element_type=jnp.float32
        ).astype(jnp.bfloat16)
        arrived = lax.all_to_all(outbox, "req", split_axis=0, concat_axis=0, tiled=True)
        rows = arrived.reshape(groups * capacity, model_width)
        gate_up = jnp.einsum(
            "md,dcf->mcf", rows, expert_gate_up[expert], preferred_element_type=jnp.float32
        )
        act = (jax.nn.silu(gate_up[:, 0]) * gate_up[:, 1]).astype(jnp.bfloat16)
        partial_value = jnp.dot(act, expert_down[expert], preferred_element_type=jnp.float32)
        outputs = partial_value.astype(jnp.bfloat16).reshape(groups, capacity, model_width)
        returns.append(lax.all_to_all(outputs, "req", split_axis=0, concat_axis=0, tiled=True))

    chosen = jnp.sum(
        jnp.where(routes[:, :, None] == expert_ids[None, None, :], logits[:, None, :], 0.0), axis=-1
    )
    gate_values = jax.nn.sigmoid(chosen)
    gate_values = gate_values / jnp.sum(gate_values, axis=1, keepdims=True)
    weights = jnp.sum(jnp.where(hit, gate_values[:, :, None], 0.0), axis=1)
    weights = weights.reshape(row_count, groups, experts_local, capacity)
    weights_hi = weights.astype(jnp.bfloat16)
    weights_lo = (weights - weights_hi.astype(jnp.float32)).astype(jnp.bfloat16)
    weights_split = jnp.stack([weights_hi, weights_lo])
    routed = jnp.zeros((row_count, model_width), jnp.float32)
    for expert in range(experts_local):
        both = jnp.einsum(
            "stgc,gcd->std", weights_split[:, :, :, expert], returns[expert],
            preferred_element_type=jnp.float32,
        )
        routed = routed + both[0] + both[1]
    shared_gu = jnp.einsum(
        "td,dcf->tcf", normed_bf, shared_gate_up, preferred_element_type=jnp.float32
    )
    shared_act = (jax.nn.silu(shared_gu[:, 0]) * shared_gu[:, 1]).astype(jnp.bfloat16)
    shared_terms = jnp.dot(shared_act, shared_down, preferred_element_type=jnp.float32)
    total = (shared_terms + routed).astype(jnp.bfloat16).reshape(row_count, tp_count, part_width)
    total = lax.all_to_all(total.transpose(1, 0, 2), "tp", split_axis=0, concat_axis=0, tiled=True)
    summed = jnp.sum(total.astype(jnp.float32), axis=0)
    return (hidden_part + summed).astype(jnp.bfloat16)


def solution(mesh):
    in_specs = (
        P("req", "tp"),
        P("req", "tp"),
        P("req", "tp"),
        P("req", None, "tp"),
        P("req", None, "tp"),
        P("req", None),
        P("req"),
        P("req", None),
        P("req", None),
        P("tp", None),
        P(),
        P(),
        P("req", None),
        P("req", None, None, "tp"),
        P("req", "tp", None),
        P(None, None, "tp"),
        P("tp", None),
    )
    out_specs = P("req", "tp")
    return jax.shard_map(shards, mesh=mesh, in_specs=in_specs, out_specs=out_specs, check_vma=False)
```

```python
import math

import jax
import jax.numpy as jnp
from jax import lax
from jax.sharding import PartitionSpec as P

QH = 20
KVH = 4
HD = 128


EPSILON = 1e-06
NEGATIVE = -1e30


def rounded(values):
    return lax.optimization_barrier(values.astype(jnp.bfloat16)).astype(jnp.float32)


def ancestors(parents):
    tree_size = parents.shape[-1]
    position = jnp.arange(tree_size, dtype=jnp.int32)
    adjacency = (parents[..., :, None] == position[None, :]) | (
        position[:, None] == position[None, :]
    )
    closure = adjacency.astype(jnp.float32)
    for doubling in range(max(1, (tree_size - 1).bit_length())):
        closure = jnp.minimum(
            jnp.einsum("...ij,...jk->...ik", closure, closure, precision=lax.Precision.HIGHEST), 1.0
        )
    return closure > 0.5


def tree_attention(queries, cache_keys, cache_values, new_keys, new_values, lengths, allowed):
    scaling = 1.0 / math.sqrt(queries.shape[-1])
    cache_scores = (
        jnp.einsum("rtkgd,rckd->rkgtc", queries, cache_keys, preferred_element_type=jnp.float32)
        * scaling
    )
    tree_scores = (
        jnp.einsum("rtkgd,rskd->rkgts", queries, new_keys, preferred_element_type=jnp.float32)
        * scaling
    )
    live = jnp.arange(cache_keys.shape[1], dtype=jnp.int32)[None, :] < lengths[:, None]
    cache_scores = jnp.where(live[:, None, None, None, :], cache_scores, NEGATIVE)
    tree_scores = jnp.where(allowed[:, None, None, :, :], tree_scores, NEGATIVE)
    highest = jnp.maximum(jnp.max(cache_scores, axis=-1), jnp.max(tree_scores, axis=-1))[..., None]
    cache_exp = jnp.exp(cache_scores - highest)
    tree_exp = jnp.exp(tree_scores - highest)
    denominator = (jnp.sum(cache_exp, axis=-1) + jnp.sum(tree_exp, axis=-1))[..., None]
    cache_probs = (cache_exp / denominator).astype(jnp.bfloat16)
    tree_probs = (tree_exp / denominator).astype(jnp.bfloat16)
    mixed = jnp.einsum(
        "rkgtc,rckd->rtkgd", cache_probs, cache_values, preferred_element_type=jnp.float32
    )
    mixed = mixed + jnp.einsum(
        "rkgts,rskd->rtkgd", tree_probs, new_values, preferred_element_type=jnp.float32
    )
    return mixed.astype(jnp.bfloat16).reshape(queries.shape[0], queries.shape[1], -1)


def shards(
    queries,
    new_keys,
    new_values,
    key_pages,
    value_pages,
    page_table,
    cache_lengths,
    parents,
    residual,
    out_weight,
    norm_gain,
    router_weight,
    routes,
    expert_gate_up,
    expert_down,
    shared_gate_up,
    shared_down,
):
    groups = lax.axis_size("req")
    tp_count = lax.axis_size("tp")
    requests = parents.shape[0]
    tree_size = parents.shape[1]
    row_count = requests * tree_size
    kv_local = new_keys.shape[1] // HD
    head_ratio = QH // KVH
    model_width = residual.shape[1]
    part_width = model_width // tp_count
    pages_dev = key_pages.shape[0]
    local_pages = page_table - lax.axis_index("req") * pages_dev
    cache_keys = key_pages[local_pages].reshape(requests, -1, kv_local, HD)
    cache_values = value_pages[local_pages].reshape(requests, -1, kv_local, HD)
    head_outputs = tree_attention(
        queries.reshape(requests, tree_size, kv_local, head_ratio, HD),
        cache_keys,
        cache_values,
        new_keys.reshape(requests, tree_size, kv_local, HD),
        new_values.reshape(requests, tree_size, kv_local, HD),
        cache_lengths,
        ancestors(parents),
    )
    attn_terms = jnp.dot(
        head_outputs.reshape(row_count, -1), out_weight, preferred_element_type=jnp.float32
    )
    column = lax.axis_index("tp") * part_width
    experts_local = expert_gate_up.shape[0]
    top_count = routes.shape[1]
    expert_count = experts_local * groups
    capacity = max(10 * requests, row_count * top_count * 5 // (4 * expert_count) + 1)
    capacity = -(-capacity // 16) * 16
    slot_count = expert_count * capacity

    flat_expert = routes.reshape(-1)
    expert_ids = jnp.arange(expert_count, dtype=jnp.int32)
    onehot = (flat_expert[:, None] == expert_ids[None, :]).astype(jnp.int32)
    earlier = jnp.cumsum(onehot, axis=0) - onehot
    rank = jnp.sum(earlier * onehot, axis=1)
    slot = (flat_expert * capacity + rank).reshape(row_count, top_count)
    slot_ids = jnp.arange(slot_count, dtype=jnp.int32)
    hit = slot[:, :, None] == slot_ids[None, None, :]

    attn_blocks = attn_terms.astype(jnp.bfloat16).reshape(row_count, tp_count, part_width)
    attn_blocks = lax.all_to_all(
        attn_blocks.transpose(1, 0, 2), "tp", split_axis=0, concat_axis=0, tiled=True
    )
    attn_part = jnp.sum(attn_blocks.astype(jnp.float32), axis=0)
    residual_part = lax.dynamic_slice_in_dim(residual, column, part_width, 1)
    hidden_part_bf = (residual_part.astype(jnp.float32) + attn_part).astype(jnp.bfloat16)
    hidden_bf = lax.all_gather(hidden_part_bf[None], "tp", axis=0, tiled=True)
    hidden = hidden_bf.transpose(1, 0, 2).reshape(row_count, model_width).astype(jnp.float32)
    rstd = lax.rsqrt(jnp.mean(hidden * hidden, axis=1, keepdims=True) + EPSILON)
    normed = hidden * rstd * norm_gain
    logits = jnp.dot(normed, router_weight, precision=lax.Precision.HIGHEST)
    normed_bf = normed.astype(jnp.bfloat16)
    hidden_part = hidden_part_bf.astype(jnp.float32)

    dispatch = jnp.any(hit, axis=1).astype(jnp.bfloat16)
    dispatch = dispatch.reshape(row_count, groups, experts_local * capacity)
    outbox = jnp.einsum(
        "tgc,td->gcd", dispatch, normed_bf, preferred_element_type=jnp.float32
    ).astype(jnp.bfloat16)
    arrived = lax.all_to_all(outbox, "req", split_axis=0, concat_axis=0, tiled=True)
    arrived = arrived.reshape(groups, experts_local, capacity, model_width)
    returns = []
    for expert in range(experts_local):
        rows = arrived[:, expert].reshape(groups * capacity, model_width)
        gate_up = jnp.einsum(
            "md,dcf->mcf", rows, expert_gate_up[expert], preferred_element_type=jnp.float32
        )
        act = (jax.nn.silu(gate_up[:, 0]) * gate_up[:, 1]).astype(jnp.bfloat16)
        partial_value = jnp.dot(act, expert_down[expert], preferred_element_type=jnp.float32)
        outputs = partial_value.astype(jnp.bfloat16).reshape(groups, capacity, model_width)
        returns.append(lax.all_to_all(outputs, "req", split_axis=0, concat_axis=0, tiled=True))

    chosen = jnp.sum(
        jnp.where(routes[:, :, None] == expert_ids[None, None, :], logits[:, None, :], 0.0), axis=-1
    )
    gate_values = jax.nn.sigmoid(chosen)
    gate_values = gate_values / jnp.sum(gate_values, axis=1, keepdims=True)
    weights = jnp.sum(jnp.where(hit, gate_values[:, :, None], 0.0), axis=1)
    weights = weights.reshape(row_count, groups, experts_local, capacity)
    weights_hi = weights.astype(jnp.bfloat16)
    weights_lo = (weights - weights_hi.astype(jnp.float32)).astype(jnp.bfloat16)
    weights_split = jnp.stack([weights_hi, weights_lo])
    routed = jnp.zeros((row_count, model_width), jnp.float32)
    for expert in range(experts_local):
        both = jnp.einsum(
            "stgc,gcd->std", weights_split[:, :, :, expert], returns[expert],
            preferred_element_type=jnp.float32,
        )
        routed = routed + both[0] + both[1]
    shared_gu = jnp.einsum(
        "td,dcf->tcf", normed_bf, shared_gate_up, preferred_element_type=jnp.float32
    )
    shared_act = (jax.nn.silu(shared_gu[:, 0]) * shared_gu[:, 1]).astype(jnp.bfloat16)
    shared_terms = jnp.dot(shared_act, shared_down, preferred_element_type=jnp.float32)
    total = (shared_terms + routed).astype(jnp.bfloat16).reshape(row_count, tp_count, part_width)
    total = lax.all_to_all(total.transpose(1, 0, 2), "tp", split_axis=0, concat_axis=0, tiled=True)
    summed = jnp.sum(total.astype(jnp.float32), axis=0)
    return (hidden_part + summed).astype(jnp.bfloat16)


def solution(mesh):
    in_specs = (
        P("req", "tp"),
        P("req", "tp"),
        P("req", "tp"),
        P("req", None, "tp"),
        P("req", None, "tp"),
        P("req", None),
        P("req"),
        P("req", None),
        P("req", None),
        P("tp", None),
        P(),
        P(),
        P("req", None),
        P("req", None, None, "tp"),
        P("req", "tp", None),
        P(None, None, "tp"),
        P("tp", None),
    )
    out_specs = P("req", "tp")
    return jax.shard_map(shards, mesh=mesh, in_specs=in_specs, out_specs=out_specs, check_vma=False)
```

```python
import math

import jax
import jax.numpy as jnp
from jax import lax
from jax.sharding import PartitionSpec as P

QH = 20
KVH = 4
HD = 128


EPSILON = 1e-06
NEGATIVE = -1e30


def rounded(values):
    return lax.optimization_barrier(values.astype(jnp.bfloat16)).astype(jnp.float32)


def ancestors(parents):
    tree_size = parents.shape[-1]
    position = jnp.arange(tree_size, dtype=jnp.int32)
    adjacency = (parents[..., :, None] == position[None, :]) | (
        position[:, None] == position[None, :]
    )
    closure = adjacency.astype(jnp.float32)
    for doubling in range(max(1, (tree_size - 1).bit_length())):
        closure = jnp.minimum(
            jnp.einsum("...ij,...jk->...ik", closure, closure, precision=lax.Precision.HIGHEST), 1.0
        )
    return closure > 0.5


def tree_attention(queries, cache_keys, cache_values, new_keys, new_values, lengths, allowed):
    scaling = 1.0 / math.sqrt(queries.shape[-1])
    cache_scores = (
        jnp.einsum("rtkgd,rckd->rkgtc", queries, cache_keys, preferred_element_type=jnp.float32)
        * scaling
    )
    tree_scores = (
        jnp.einsum("rtkgd,rskd->rkgts", queries, new_keys, preferred_element_type=jnp.float32)
        * scaling
    )
    live = jnp.arange(cache_keys.shape[1], dtype=jnp.int32)[None, :] < lengths[:, None]
    cache_scores = jnp.where(live[:, None, None, None, :], cache_scores, NEGATIVE)
    tree_scores = jnp.where(allowed[:, None, None, :, :], tree_scores, NEGATIVE)
    highest = jnp.maximum(jnp.max(cache_scores, axis=-1), jnp.max(tree_scores, axis=-1))[..., None]
    cache_exp = jnp.exp(cache_scores - highest)
    tree_exp = jnp.exp(tree_scores - highest)
    denominator = (jnp.sum(cache_exp, axis=-1) + jnp.sum(tree_exp, axis=-1))[..., None]
    cache_probs = (cache_exp / denominator).astype(jnp.bfloat16)
    tree_probs = (tree_exp / denominator).astype(jnp.bfloat16)
    mixed = jnp.einsum(
        "rkgtc,rckd->rtkgd", cache_probs, cache_values, preferred_element_type=jnp.float32
    )
    mixed = mixed + jnp.einsum(
        "rkgts,rskd->rtkgd", tree_probs, new_values, preferred_element_type=jnp.float32
    )
    return mixed.astype(jnp.bfloat16).reshape(queries.shape[0], queries.shape[1], -1)


def shards(
    queries,
    new_keys,
    new_values,
    key_pages,
    value_pages,
    page_table,
    cache_lengths,
    parents,
    residual,
    out_weight,
    norm_gain,
    router_weight,
    routes,
    expert_gate_up,
    expert_down,
    shared_gate_up,
    shared_down,
):
    groups = lax.axis_size("req")
    tp_count = lax.axis_size("tp")
    requests = parents.shape[0]
    tree_size = parents.shape[1]
    row_count = requests * tree_size
    kv_local = new_keys.shape[1] // HD
    head_ratio = QH // KVH
    model_width = residual.shape[1]
    part_width = model_width // tp_count
    pages_dev = key_pages.shape[0]
    local_pages = page_table - lax.axis_index("req") * pages_dev
    cache_keys = key_pages[local_pages].reshape(requests, -1, kv_local, HD)
    cache_values = value_pages[local_pages].reshape(requests, -1, kv_local, HD)
    head_outputs = tree_attention(
        queries.reshape(requests, tree_size, kv_local, head_ratio, HD),
        cache_keys,
        cache_values,
        new_keys.reshape(requests, tree_size, kv_local, HD),
        new_values.reshape(requests, tree_size, kv_local, HD),
        cache_lengths,
        ancestors(parents),
    )
    attn_terms = jnp.dot(
        head_outputs.reshape(row_count, -1), out_weight, preferred_element_type=jnp.float32
    )
    column = lax.axis_index("tp") * part_width
    experts_local = expert_gate_up.shape[0]
    top_count = routes.shape[1]
    expert_count = experts_local * groups
    capacity = max(10 * requests, row_count * top_count * 5 // (4 * expert_count) + 1)
    capacity = -(-capacity // 16) * 16
    slot_count = expert_count * capacity

    flat_expert = routes.reshape(-1)
    expert_ids = jnp.arange(expert_count, dtype=jnp.int32)
    onehot = (flat_expert[:, None] == expert_ids[None, :]).astype(jnp.int32)
    earlier = jnp.cumsum(onehot, axis=0) - onehot
    rank = jnp.sum(earlier * onehot, axis=1)
    slot = (flat_expert * capacity + rank).reshape(row_count, top_count)
    slot_ids = jnp.arange(slot_count, dtype=jnp.int32)
    hit = slot[:, :, None] == slot_ids[None, None, :]

    attn_blocks = attn_terms.astype(jnp.bfloat16).reshape(row_count, tp_count, part_width)
    attn_blocks = lax.all_to_all(
        attn_blocks.transpose(1, 0, 2), "tp", split_axis=0, concat_axis=0, tiled=True
    )
    attn_part = jnp.sum(attn_blocks.astype(jnp.float32), axis=0)
    residual_part = lax.dynamic_slice_in_dim(residual, column, part_width, 1)
    hidden_part_bf = (residual_part.astype(jnp.float32) + attn_part).astype(jnp.bfloat16)
    hidden_bf = lax.all_gather(hidden_part_bf[None], "tp", axis=0, tiled=True)
    hidden = hidden_bf.transpose(1, 0, 2).reshape(row_count, model_width).astype(jnp.float32)
    rstd = lax.rsqrt(jnp.mean(hidden * hidden, axis=1, keepdims=True) + EPSILON)
    normed = hidden * rstd * norm_gain
    logits = jnp.dot(normed, router_weight, precision=lax.Precision.HIGHEST)
    normed_bf = normed.astype(jnp.bfloat16)
    hidden_part = hidden_part_bf.astype(jnp.float32)

    dispatch = jnp.any(hit, axis=1).astype(jnp.bfloat16)
    dispatch = dispatch.reshape(row_count, groups, experts_local, capacity)
    returns = []
    for expert in range(experts_local):
        outbox = jnp.einsum(
            "tgc,td->gcd", dispatch[:, :, expert], normed_bf, preferred_element_type=jnp.float32
        ).astype(jnp.bfloat16)
        arrived = lax.all_to_all(outbox, "req", split_axis=0, concat_axis=0, tiled=True)
        rows = arrived.reshape(groups * capacity, model_width)
        gate_up = jnp.einsum(
            "md,dcf->mcf", rows, expert_gate_up[expert], preferred_element_type=jnp.float32
        )
        act = (jax.nn.silu(gate_up[:, 0]) * gate_up[:, 1]).astype(jnp.bfloat16)
        partial_value = jnp.dot(act, expert_down[expert], preferred_element_type=jnp.float32)
        partial_bf = partial_value.astype(jnp.bfloat16)
        if expert < experts_local - 1:
            outputs = partial_bf.reshape(groups, capacity, model_width)
        else:
            outputs = lax.psum_scatter(
                partial_bf.reshape(-1, tp_count, part_width).transpose(1, 0, 2),
                "tp", scatter_dimension=0, tiled=True,
            ).reshape(groups, capacity, part_width)
        returns.append(lax.all_to_all(outputs, "req", split_axis=0, concat_axis=0, tiled=True))

    chosen = jnp.sum(
        jnp.where(routes[:, :, None] == expert_ids[None, None, :], logits[:, None, :], 0.0), axis=-1
    )
    gate_values = jax.nn.sigmoid(chosen)
    gate_values = gate_values / jnp.sum(gate_values, axis=1, keepdims=True)
    weights = jnp.sum(jnp.where(hit, gate_values[:, :, None], 0.0), axis=1)
    weights = weights.reshape(row_count, groups, experts_local, capacity)
    weights_hi = weights.astype(jnp.bfloat16)
    weights_lo = (weights - weights_hi.astype(jnp.float32)).astype(jnp.bfloat16)
    weights_split = jnp.stack([weights_hi, weights_lo])
    routed = jnp.zeros((row_count, model_width), jnp.float32)
    for expert in range(experts_local):
        both = jnp.einsum(
            "stgc,gcd->std", weights_split[:, :, :, expert], returns[expert],
            preferred_element_type=jnp.float32,
        )
        if expert < experts_local - 1:
            routed = routed + both[0] + both[1]
        else:
            routed_last = both[0] + both[1]

    shared_gu = jnp.einsum(
        "td,dcf->tcf", normed_bf, shared_gate_up, preferred_element_type=jnp.float32
    )
    shared_act = (jax.nn.silu(shared_gu[:, 0]) * shared_gu[:, 1]).astype(jnp.bfloat16)
    shared_terms = jnp.dot(shared_act, shared_down, preferred_element_type=jnp.float32)
    total = (shared_terms + routed).astype(jnp.bfloat16).reshape(row_count, tp_count, part_width)
    total = lax.all_to_all(total.transpose(1, 0, 2), "tp", split_axis=0, concat_axis=0, tiled=True)
    summed = jnp.sum(total.astype(jnp.float32), axis=0) + routed_last
    return (hidden_part + summed).astype(jnp.bfloat16)


def solution(mesh):
    in_specs = (
        P("req", "tp"),
        P("req", "tp"),
        P("req", "tp"),
        P("req", None, "tp"),
        P("req", None, "tp"),
        P("req", None),
        P("req"),
        P("req", None),
        P("req", None),
        P("tp", None),
        P(),
        P(),
        P("req", None),
        P("req", None, None, "tp"),
        P("req", "tp", None),
        P(None, None, "tp"),
        P("tp", None),
    )
    out_specs = P("req", "tp")
    return jax.shard_map(shards, mesh=mesh, in_specs=in_specs, out_specs=out_specs, check_vma=False)
```

```python
import math

import jax
import jax.numpy as jnp
from jax import lax
from jax.sharding import PartitionSpec as P

QH = 20
KVH = 4
HD = 128


EPSILON = 1e-06
NEGATIVE = -1e30


def rounded(values):
    return lax.optimization_barrier(values.astype(jnp.bfloat16)).astype(jnp.float32)


def ancestors(parents):
    tree_size = parents.shape[-1]
    position = jnp.arange(tree_size, dtype=jnp.int32)
    adjacency = (parents[..., :, None] == position[None, :]) | (
        position[:, None] == position[None, :]
    )
    closure = adjacency.astype(jnp.float32)
    for doubling in range(max(1, (tree_size - 1).bit_length())):
        closure = jnp.minimum(
            jnp.einsum("...ij,...jk->...ik", closure, closure, precision=lax.Precision.HIGHEST), 1.0
        )
    return closure > 0.5


def tree_attention(queries, cache_keys, cache_values, new_keys, new_values, lengths, allowed):
    scaling = 1.0 / math.sqrt(queries.shape[-1])
    cache_scores = (
        jnp.einsum("rtkgd,rckd->rkgtc", queries, cache_keys, preferred_element_type=jnp.float32)
        * scaling
    )
    tree_scores = (
        jnp.einsum("rtkgd,rskd->rkgts", queries, new_keys, preferred_element_type=jnp.float32)
        * scaling
    )
    live = jnp.arange(cache_keys.shape[1], dtype=jnp.int32)[None, :] < lengths[:, None]
    cache_scores = jnp.where(live[:, None, None, None, :], cache_scores, NEGATIVE)
    tree_scores = jnp.where(allowed[:, None, None, :, :], tree_scores, NEGATIVE)
    highest = jnp.maximum(jnp.max(cache_scores, axis=-1), jnp.max(tree_scores, axis=-1))[..., None]
    cache_exp = jnp.exp(cache_scores - highest)
    tree_exp = jnp.exp(tree_scores - highest)
    denominator = (jnp.sum(cache_exp, axis=-1) + jnp.sum(tree_exp, axis=-1))[..., None]
    cache_probs = (cache_exp / denominator).astype(jnp.bfloat16)
    tree_probs = (tree_exp / denominator).astype(jnp.bfloat16)
    mixed = jnp.einsum(
        "rkgtc,rckd->rtkgd", cache_probs, cache_values, preferred_element_type=jnp.float32
    )
    mixed = mixed + jnp.einsum(
        "rkgts,rskd->rtkgd", tree_probs, new_values, preferred_element_type=jnp.float32
    )
    return mixed.astype(jnp.bfloat16).reshape(queries.shape[0], queries.shape[1], -1)


def shards(
    queries,
    new_keys,
    new_values,
    key_pages,
    value_pages,
    page_table,
    cache_lengths,
    parents,
    residual,
    out_weight,
    norm_gain,
    router_weight,
    routes,
    expert_gate_up,
    expert_down,
    shared_gate_up,
    shared_down,
):
    groups = lax.axis_size("req")
    tp_count = lax.axis_size("tp")
    requests = parents.shape[0]
    tree_size = parents.shape[1]
    row_count = requests * tree_size
    kv_local = new_keys.shape[1] // HD
    head_ratio = QH // KVH
    model_width = residual.shape[1]
    part_width = model_width // tp_count
    pages_dev = key_pages.shape[0]
    local_pages = page_table - lax.axis_index("req") * pages_dev
    cache_keys = key_pages[local_pages].reshape(requests, -1, kv_local, HD)
    cache_values = value_pages[local_pages].reshape(requests, -1, kv_local, HD)
    head_outputs = tree_attention(
        queries.reshape(requests, tree_size, kv_local, head_ratio, HD),
        cache_keys,
        cache_values,
        new_keys.reshape(requests, tree_size, kv_local, HD),
        new_values.reshape(requests, tree_size, kv_local, HD),
        cache_lengths,
        ancestors(parents),
    )
    attn_terms = jnp.dot(
        head_outputs.reshape(row_count, -1), out_weight, preferred_element_type=jnp.float32
    )
    column = lax.axis_index("tp") * part_width
    experts_local = expert_gate_up.shape[0]
    top_count = routes.shape[1]
    expert_count = experts_local * groups
    capacity = max(10 * requests, row_count * top_count * 5 // (4 * expert_count) + 1)
    capacity = -(-capacity // 16) * 16
    slot_count = expert_count * capacity

    flat_expert = routes.reshape(-1)
    expert_ids = jnp.arange(expert_count, dtype=jnp.int32)
    onehot = (flat_expert[:, None] == expert_ids[None, :]).astype(jnp.int32)
    earlier = jnp.cumsum(onehot, axis=0) - onehot
    rank = jnp.sum(earlier * onehot, axis=1)
    slot = (flat_expert * capacity + rank).reshape(row_count, top_count)
    slot_ids = jnp.arange(slot_count, dtype=jnp.int32)
    hit = slot[:, :, None] == slot_ids[None, None, :]

    attn_blocks = attn_terms.astype(jnp.bfloat16).reshape(row_count, tp_count, part_width)
    attn_blocks = lax.all_to_all(
        attn_blocks.transpose(1, 0, 2), "tp", split_axis=0, concat_axis=0, tiled=True
    )
    attn_part = jnp.sum(attn_blocks.astype(jnp.float32), axis=0)
    residual_part = lax.dynamic_slice_in_dim(residual, column, part_width, 1)
    hidden_part_bf = (residual_part.astype(jnp.float32) + attn_part).astype(jnp.bfloat16)
    hidden_bf = lax.all_gather(hidden_part_bf[None], "tp", axis=0, tiled=True)
    hidden = hidden_bf.transpose(1, 0, 2).reshape(row_count, model_width).astype(jnp.float32)
    rstd = lax.rsqrt(jnp.mean(hidden * hidden, axis=1, keepdims=True) + EPSILON)
    normed = hidden * rstd * norm_gain
    logits = jnp.dot(normed, router_weight, precision=lax.Precision.HIGHEST)
    normed_bf = normed.astype(jnp.bfloat16)
    hidden_part = hidden_part_bf.astype(jnp.float32)

    dispatch = jnp.any(hit, axis=1).astype(jnp.bfloat16)
    dispatch = dispatch.reshape(row_count, groups, experts_local, capacity)
    returns = []
    for expert in range(experts_local):
        outbox = jnp.einsum(
            "tgc,td->gcd", dispatch[:, :, expert], normed_bf, preferred_element_type=jnp.float32
        ).astype(jnp.bfloat16)
        arrived = lax.all_to_all(outbox, "req", split_axis=0, concat_axis=0, tiled=True)
        rows = arrived.reshape(groups * capacity, model_width)
        gate_up = jnp.einsum(
            "md,dcf->mcf", rows, expert_gate_up[expert], preferred_element_type=jnp.float32
        )
        act = (jax.nn.silu(gate_up[:, 0]) * gate_up[:, 1]).astype(jnp.bfloat16)
        partial_value = jnp.dot(act, expert_down[expert], preferred_element_type=jnp.float32)
        partial_bf = partial_value.astype(jnp.bfloat16)
        if expert < experts_local - 1:
            outputs = partial_bf.reshape(groups, capacity, model_width)
        else:
            outputs = lax.psum_scatter(
                partial_bf.reshape(-1, tp_count, part_width).transpose(1, 0, 2),
                "tp", scatter_dimension=0, tiled=True,
            ).reshape(groups, capacity, part_width)
        returns.append(lax.all_to_all(outputs, "req", split_axis=0, concat_axis=0, tiled=True))

    chosen = jnp.sum(
        jnp.where(routes[:, :, None] == expert_ids[None, None, :], logits[:, None, :], 0.0), axis=-1
    )
    gate_values = jax.nn.sigmoid(chosen)
    gate_values = gate_values / jnp.sum(gate_values, axis=1, keepdims=True)
    weights = jnp.sum(jnp.where(hit, gate_values[:, :, None], 0.0), axis=1)
    weights = weights.reshape(row_count, groups, experts_local, capacity)
    weights_hi = weights.astype(jnp.bfloat16)
    weights_lo = (weights - weights_hi.astype(jnp.float32)).astype(jnp.bfloat16)
    weights_split = jnp.stack([weights_hi, weights_lo])
    routed = jnp.zeros((row_count, model_width), jnp.float32)
    for expert in range(experts_local):
        both = jnp.einsum(
            "stgc,gcd->std", weights_split[:, :, :, expert], returns[expert],
            preferred_element_type=jnp.float32,
        )
        if expert < experts_local - 1:
            routed = routed + both[0] + both[1]
        else:
            routed_last = both[0] + both[1]

    shared_gu = jnp.einsum(
        "td,dcf->tcf", normed_bf, shared_gate_up, preferred_element_type=jnp.float32
    )
    shared_act = (jax.nn.silu(shared_gu[:, 0]) * shared_gu[:, 1]).astype(jnp.bfloat16)
    shared_terms = jnp.dot(shared_act, shared_down, preferred_element_type=jnp.float32)
    total = (shared_terms + routed).astype(jnp.bfloat16).reshape(row_count, tp_count, part_width)
    summed = lax.psum_scatter(total.transpose(1, 0, 2), "tp", scatter_dimension=0, tiled=True)
    summed = summed[0].astype(jnp.float32) + routed_last
    return (hidden_part + summed).astype(jnp.bfloat16)


def solution(mesh):
    in_specs = (
        P("req", "tp"),
        P("req", "tp"),
        P("req", "tp"),
        P("req", None, "tp"),
        P("req", None, "tp"),
        P("req", None),
        P("req"),
        P("req", None),
        P("req", None),
        P("tp", None),
        P(),
        P(),
        P("req", None),
        P("req", None, None, "tp"),
        P("req", "tp", None),
        P(None, None, "tp"),
        P("tp", None),
    )
    out_specs = P("req", "tp")
    return jax.shard_map(shards, mesh=mesh, in_specs=in_specs, out_specs=out_specs, check_vma=False)
```

```python
import math

import jax
import jax.numpy as jnp
from jax import lax
from jax.sharding import PartitionSpec as P

QH = 20
KVH = 4
HD = 128


EPSILON = 1e-06
NEGATIVE = -1e30


def rounded(values):
    return lax.optimization_barrier(values.astype(jnp.bfloat16)).astype(jnp.float32)


def ancestors(parents):
    tree_size = parents.shape[-1]
    position = jnp.arange(tree_size, dtype=jnp.int32)
    adjacency = (parents[..., :, None] == position[None, :]) | (
        position[:, None] == position[None, :]
    )
    closure = adjacency.astype(jnp.float32)
    for doubling in range(max(1, (tree_size - 1).bit_length())):
        closure = jnp.minimum(
            jnp.einsum("...ij,...jk->...ik", closure, closure, precision=lax.Precision.HIGHEST), 1.0
        )
    return closure > 0.5


def tree_attention(queries, cache_keys, cache_values, new_keys, new_values, lengths, allowed):
    scaling = 1.0 / math.sqrt(queries.shape[-1])
    cache_scores = (
        jnp.einsum("rtkgd,rckd->rkgtc", queries, cache_keys, preferred_element_type=jnp.float32)
        * scaling
    )
    tree_scores = (
        jnp.einsum("rtkgd,rskd->rkgts", queries, new_keys, preferred_element_type=jnp.float32)
        * scaling
    )
    live = jnp.arange(cache_keys.shape[1], dtype=jnp.int32)[None, :] < lengths[:, None]
    cache_scores = jnp.where(live[:, None, None, None, :], cache_scores, NEGATIVE)
    tree_scores = jnp.where(allowed[:, None, None, :, :], tree_scores, NEGATIVE)
    highest = jnp.maximum(jnp.max(cache_scores, axis=-1), jnp.max(tree_scores, axis=-1))[..., None]
    cache_exp = jnp.exp(cache_scores - highest)
    tree_exp = jnp.exp(tree_scores - highest)
    denominator = (jnp.sum(cache_exp, axis=-1) + jnp.sum(tree_exp, axis=-1))[..., None]
    cache_probs = (cache_exp / denominator).astype(jnp.bfloat16)
    tree_probs = (tree_exp / denominator).astype(jnp.bfloat16)
    mixed = jnp.einsum(
        "rkgtc,rckd->rtkgd", cache_probs, cache_values, preferred_element_type=jnp.float32
    )
    mixed = mixed + jnp.einsum(
        "rkgts,rskd->rtkgd", tree_probs, new_values, preferred_element_type=jnp.float32
    )
    return mixed.astype(jnp.bfloat16).reshape(queries.shape[0], queries.shape[1], -1)


def shards(
    queries,
    new_keys,
    new_values,
    key_pages,
    value_pages,
    page_table,
    cache_lengths,
    parents,
    residual,
    out_weight,
    norm_gain,
    router_weight,
    routes,
    expert_gate_up,
    expert_down,
    shared_gate_up,
    shared_down,
):
    groups = lax.axis_size("req")
    tp_count = lax.axis_size("tp")
    requests = parents.shape[0]
    tree_size = parents.shape[1]
    row_count = requests * tree_size
    kv_local = new_keys.shape[1] // HD
    head_ratio = QH // KVH
    model_width = residual.shape[1]
    part_width = model_width // tp_count
    pages_dev = key_pages.shape[0]
    local_pages = page_table - lax.axis_index("req") * pages_dev
    allowed = ancestors(parents)
    column = lax.axis_index("tp") * part_width
    half = requests // 2
    attn_parts = []
    for first, count in ((0, half), (half, requests - half)):
        rows = slice(first * tree_size, (first + count) * tree_size)
        pages = local_pages[first : first + count]
        head_outputs = tree_attention(
            queries[rows].reshape(count, tree_size, kv_local, head_ratio, HD),
            key_pages[pages].reshape(count, -1, kv_local, HD),
            value_pages[pages].reshape(count, -1, kv_local, HD),
            new_keys[rows].reshape(count, tree_size, kv_local, HD),
            new_values[rows].reshape(count, tree_size, kv_local, HD),
            cache_lengths[first : first + count],
            allowed[first : first + count],
        )
        attn_terms = jnp.dot(
            head_outputs.reshape(count * tree_size, -1), out_weight,
            preferred_element_type=jnp.float32,
        )
        attn_blocks = attn_terms.astype(jnp.bfloat16).reshape(-1, tp_count, part_width)
        attn_blocks = attn_blocks.transpose(1, 0, 2)
        if first == 0:
            attn_sum = lax.psum_scatter(attn_blocks, "tp", scatter_dimension=0, tiled=True)[0]
            attn_parts.append(attn_sum.astype(jnp.float32))
        else:
            attn_blocks = lax.all_to_all(attn_blocks, "tp", split_axis=0, concat_axis=0, tiled=True)
            attn_parts.append(jnp.sum(attn_blocks.astype(jnp.float32), axis=0))
    attn_part = jnp.concatenate(attn_parts, axis=0)
    column = lax.axis_index("tp") * part_width
    experts_local = expert_gate_up.shape[0]
    top_count = routes.shape[1]
    expert_count = experts_local * groups
    capacity = max(10 * requests, row_count * top_count * 5 // (4 * expert_count) + 1)
    capacity = -(-capacity // 16) * 16
    slot_count = expert_count * capacity

    flat_expert = routes.reshape(-1)
    expert_ids = jnp.arange(expert_count, dtype=jnp.int32)
    onehot = (flat_expert[:, None] == expert_ids[None, :]).astype(jnp.int32)
    earlier = jnp.cumsum(onehot, axis=0) - onehot
    rank = jnp.sum(earlier * onehot, axis=1)
    slot = (flat_expert * capacity + rank).reshape(row_count, top_count)
    slot_ids = jnp.arange(slot_count, dtype=jnp.int32)
    hit = slot[:, :, None] == slot_ids[None, None, :]

    residual_part = lax.dynamic_slice_in_dim(residual, column, part_width, 1)
    hidden_part_bf = (residual_part.astype(jnp.float32) + attn_part).astype(jnp.bfloat16)
    hidden = lax.all_gather(hidden_part_bf, "tp", axis=1, tiled=True).astype(jnp.float32)
    rstd = lax.rsqrt(jnp.mean(hidden * hidden, axis=1, keepdims=True) + EPSILON)
    normed = hidden * rstd * norm_gain
    logits = jnp.dot(normed, router_weight, precision=lax.Precision.HIGHEST)
    normed_bf = normed.astype(jnp.bfloat16)
    hidden_part = hidden_part_bf.astype(jnp.float32)

    dispatch = jnp.any(hit, axis=1).astype(jnp.bfloat16)
    dispatch = dispatch.reshape(row_count, groups, experts_local, capacity)
    returns = []
    for expert in range(experts_local):
        outbox = jnp.einsum(
            "tgc,td->gcd", dispatch[:, :, expert], normed_bf, preferred_element_type=jnp.float32
        ).astype(jnp.bfloat16)
        arrived = lax.all_to_all(outbox, "req", split_axis=0, concat_axis=0, tiled=True)
        rows = arrived.reshape(groups * capacity, model_width)
        gate_up = jnp.einsum(
            "md,dcf->mcf", rows, expert_gate_up[expert], preferred_element_type=jnp.float32
        )
        act = (jax.nn.silu(gate_up[:, 0]) * gate_up[:, 1]).astype(jnp.bfloat16)
        partial_value = jnp.dot(act, expert_down[expert], preferred_element_type=jnp.float32)
        partial_bf = partial_value.astype(jnp.bfloat16)
        if expert < experts_local - 1:
            outputs = partial_bf.reshape(groups, capacity, model_width)
        else:
            outputs = lax.psum_scatter(
                partial_bf.reshape(-1, tp_count, part_width).transpose(1, 0, 2),
                "tp", scatter_dimension=0, tiled=True,
            ).reshape(groups, capacity, part_width)
        returns.append(lax.all_to_all(outputs, "req", split_axis=0, concat_axis=0, tiled=True))

    chosen = jnp.sum(
        jnp.where(routes[:, :, None] == expert_ids[None, None, :], logits[:, None, :], 0.0), axis=-1
    )
    gate_values = jax.nn.sigmoid(chosen)
    gate_values = gate_values / jnp.sum(gate_values, axis=1, keepdims=True)
    weights = jnp.sum(jnp.where(hit, gate_values[:, :, None], 0.0), axis=1)
    weights = weights.reshape(row_count, groups, experts_local, capacity)
    weights_hi = weights.astype(jnp.bfloat16)
    weights_lo = (weights - weights_hi.astype(jnp.float32)).astype(jnp.bfloat16)
    weights_split = jnp.stack([weights_hi, weights_lo])
    routed = jnp.zeros((row_count, model_width), jnp.float32)
    for expert in range(experts_local):
        both = jnp.einsum(
            "stgc,gcd->std", weights_split[:, :, :, expert], returns[expert],
            preferred_element_type=jnp.float32,
        )
        if expert < experts_local - 1:
            routed = routed + both[0] + both[1]
        else:
            routed_last = both[0] + both[1]

    shared_gu = jnp.einsum(
        "td,dcf->tcf", normed_bf, shared_gate_up, preferred_element_type=jnp.float32
    )
    shared_act = (jax.nn.silu(shared_gu[:, 0]) * shared_gu[:, 1]).astype(jnp.bfloat16)
    shared_terms = jnp.dot(shared_act, shared_down, preferred_element_type=jnp.float32)
    total = (shared_terms + routed).astype(jnp.bfloat16).reshape(row_count, tp_count, part_width)
    summed = lax.psum_scatter(total.transpose(1, 0, 2), "tp", scatter_dimension=0, tiled=True)
    summed = summed[0].astype(jnp.float32) + routed_last
    return (hidden_part + summed).astype(jnp.bfloat16)


def solution(mesh):
    in_specs = (
        P("req", "tp"),
        P("req", "tp"),
        P("req", "tp"),
        P("req", None, "tp"),
        P("req", None, "tp"),
        P("req", None),
        P("req"),
        P("req", None),
        P("req", None),
        P("tp", None),
        P(),
        P(),
        P("req", None),
        P("req", None, None, "tp"),
        P("req", "tp", None),
        P(None, None, "tp"),
        P("tp", None),
    )
    out_specs = P("req", "tp")
    return jax.shard_map(shards, mesh=mesh, in_specs=in_specs, out_specs=out_specs, check_vma=False)
```

```python
import math

import jax
import jax.numpy as jnp
from jax import lax
from jax.sharding import PartitionSpec as P

QH = 20
KVH = 4
HD = 128


EPSILON = 1e-06
NEGATIVE = -1e30


def rounded(values):
    return lax.optimization_barrier(values.astype(jnp.bfloat16)).astype(jnp.float32)


def ancestors(parents):
    tree_size = parents.shape[-1]
    position = jnp.arange(tree_size, dtype=jnp.int32)
    adjacency = (parents[..., :, None] == position[None, :]) | (
        position[:, None] == position[None, :]
    )
    closure = adjacency.astype(jnp.float32)

    def doubling(step, closure):
        return jnp.minimum(
            jnp.einsum("...ij,...jk->...ik", closure, closure, precision=lax.Precision.HIGHEST), 1.0
        )

    closure = lax.fori_loop(0, max(1, (tree_size - 1).bit_length()), doubling, closure)
    return closure > 0.5


def tree_attention(queries, cache_keys, cache_values, new_keys, new_values, lengths, allowed):
    scaling = 1.0 / math.sqrt(queries.shape[-1])
    cache_scores = (
        jnp.einsum("rtkgd,rckd->rkgtc", queries, cache_keys, preferred_element_type=jnp.float32)
        * scaling
    )
    tree_scores = (
        jnp.einsum("rtkgd,rskd->rkgts", queries, new_keys, preferred_element_type=jnp.float32)
        * scaling
    )
    live = jnp.arange(cache_keys.shape[1], dtype=jnp.int32)[None, :] < lengths[:, None]
    cache_scores = jnp.where(live[:, None, None, None, :], cache_scores, NEGATIVE)
    tree_scores = jnp.where(allowed[:, None, None, :, :], tree_scores, NEGATIVE)
    highest = jnp.maximum(jnp.max(cache_scores, axis=-1), jnp.max(tree_scores, axis=-1))[..., None]
    cache_exp = jnp.exp(cache_scores - highest)
    tree_exp = jnp.exp(tree_scores - highest)
    denominator = (jnp.sum(cache_exp, axis=-1) + jnp.sum(tree_exp, axis=-1))[..., None]
    cache_probs = (cache_exp / denominator).astype(jnp.bfloat16)
    tree_probs = (tree_exp / denominator).astype(jnp.bfloat16)
    mixed = jnp.einsum(
        "rkgtc,rckd->rtkgd", cache_probs, cache_values, preferred_element_type=jnp.float32
    )
    mixed = mixed + jnp.einsum(
        "rkgts,rskd->rtkgd", tree_probs, new_values, preferred_element_type=jnp.float32
    )
    return mixed.astype(jnp.bfloat16).reshape(queries.shape[0], queries.shape[1], -1)


def shards(
    queries,
    new_keys,
    new_values,
    key_pages,
    value_pages,
    page_table,
    cache_lengths,
    parents,
    residual,
    out_weight,
    norm_gain,
    router_weight,
    routes,
    expert_gate_up,
    expert_down,
    shared_gate_up,
    shared_down,
):
    groups = lax.axis_size("req")
    tp_count = lax.axis_size("tp")
    requests = parents.shape[0]
    tree_size = parents.shape[1]
    row_count = requests * tree_size
    kv_local = new_keys.shape[1] // HD
    head_ratio = QH // KVH
    model_width = residual.shape[1]
    part_width = model_width // tp_count
    pages_dev = key_pages.shape[0]
    local_pages = page_table - lax.axis_index("req") * pages_dev
    cache_keys = key_pages[local_pages].reshape(requests, -1, kv_local, HD)
    cache_values = value_pages[local_pages].reshape(requests, -1, kv_local, HD)
    head_outputs = tree_attention(
        queries.reshape(requests, tree_size, kv_local, head_ratio, HD),
        cache_keys,
        cache_values,
        new_keys.reshape(requests, tree_size, kv_local, HD),
        new_values.reshape(requests, tree_size, kv_local, HD),
        cache_lengths,
        ancestors(parents),
    )
    attn_terms = jnp.dot(
        head_outputs.reshape(row_count, -1), out_weight, preferred_element_type=jnp.float32
    )
    column = lax.axis_index("tp") * part_width
    experts_local = expert_gate_up.shape[0]
    top_count = routes.shape[1]
    expert_count = experts_local * groups
    capacity = max(10 * requests, row_count * top_count * 5 // (4 * expert_count) + 1)
    capacity = -(-capacity // 16) * 16
    slot_count = expert_count * capacity

    flat_expert = routes.reshape(-1)
    expert_ids = jnp.arange(expert_count, dtype=jnp.int32)
    onehot = (flat_expert[:, None] == expert_ids[None, :]).astype(jnp.int32)
    earlier = jnp.cumsum(onehot, axis=0) - onehot
    rank = jnp.sum(earlier * onehot, axis=1)
    slot = (flat_expert * capacity + rank).reshape(row_count, top_count)
    slot_ids = jnp.arange(slot_count, dtype=jnp.int32)
    hit = slot[:, :, None] == slot_ids[None, None, :]

    attn_blocks = attn_terms.astype(jnp.bfloat16).reshape(row_count, tp_count, part_width)
    attn_blocks = lax.all_to_all(
        attn_blocks.transpose(1, 0, 2), "tp", split_axis=0, concat_axis=0, tiled=True
    )
    attn_part = jnp.sum(attn_blocks.astype(jnp.float32), axis=0)
    residual_part = lax.dynamic_slice_in_dim(residual, column, part_width, 1)
    hidden_part_bf = (residual_part.astype(jnp.float32) + attn_part).astype(jnp.bfloat16)
    hidden = lax.all_gather(hidden_part_bf, "tp", axis=1, tiled=True).astype(jnp.float32)
    rstd = lax.rsqrt(jnp.mean(hidden * hidden, axis=1, keepdims=True) + EPSILON)
    normed = hidden * rstd * norm_gain
    logits = jnp.dot(normed, router_weight, precision=lax.Precision.HIGHEST)
    normed_bf = normed.astype(jnp.bfloat16)
    hidden_part = hidden_part_bf.astype(jnp.float32)

    dispatch = jnp.any(hit, axis=1).astype(jnp.bfloat16)
    dispatch = dispatch.reshape(row_count, groups, experts_local, capacity)
    returns = []
    for expert in range(experts_local):
        outbox = jnp.einsum(
            "tgc,td->gcd", dispatch[:, :, expert], normed_bf, preferred_element_type=jnp.float32
        ).astype(jnp.bfloat16)
        arrived = lax.all_to_all(outbox, "req", split_axis=0, concat_axis=0, tiled=True)
        rows = arrived.reshape(groups * capacity, model_width)
        gate_up = jnp.einsum(
            "md,dcf->mcf", rows, expert_gate_up[expert], preferred_element_type=jnp.float32
        )
        act = (jax.nn.silu(gate_up[:, 0]) * gate_up[:, 1]).astype(jnp.bfloat16)
        partial_value = jnp.dot(act, expert_down[expert], preferred_element_type=jnp.float32)
        partial_bf = partial_value.astype(jnp.bfloat16)
        if expert < experts_local - 1:
            outputs = partial_bf.reshape(groups, capacity, model_width)
        else:
            outputs = lax.psum_scatter(
                partial_bf.reshape(-1, tp_count, part_width).transpose(1, 0, 2),
                "tp", scatter_dimension=0, tiled=True,
            ).reshape(groups, capacity, part_width)
        returns.append(lax.all_to_all(outputs, "req", split_axis=0, concat_axis=0, tiled=True))

    chosen = jnp.sum(
        jnp.where(routes[:, :, None] == expert_ids[None, None, :], logits[:, None, :], 0.0), axis=-1
    )
    gate_values = jax.nn.sigmoid(chosen)
    gate_values = gate_values / jnp.sum(gate_values, axis=1, keepdims=True)
    weights = jnp.sum(jnp.where(hit, gate_values[:, :, None], 0.0), axis=1)
    weights = weights.reshape(row_count, groups, experts_local, capacity)
    weights_hi = weights.astype(jnp.bfloat16)
    weights_lo = (weights - weights_hi.astype(jnp.float32)).astype(jnp.bfloat16)
    weights_split = jnp.stack([weights_hi, weights_lo])
    routed = jnp.zeros((row_count, model_width), jnp.float32)
    for expert in range(experts_local):
        both = jnp.einsum(
            "stgc,gcd->std", weights_split[:, :, :, expert], returns[expert],
            preferred_element_type=jnp.float32,
        )
        if expert < experts_local - 1:
            routed = routed + both[0] + both[1]
        else:
            routed_last = both[0] + both[1]

    shared_gu = jnp.einsum(
        "td,dcf->tcf", normed_bf, shared_gate_up, preferred_element_type=jnp.float32
    )
    shared_act = (jax.nn.silu(shared_gu[:, 0]) * shared_gu[:, 1]).astype(jnp.bfloat16)
    shared_terms = jnp.dot(shared_act, shared_down, preferred_element_type=jnp.float32)
    total = (shared_terms + routed).astype(jnp.bfloat16).reshape(row_count, tp_count, part_width)
    summed = lax.psum_scatter(total.transpose(1, 0, 2), "tp", scatter_dimension=0, tiled=True)
    summed = summed[0].astype(jnp.float32) + routed_last
    return (hidden_part + summed).astype(jnp.bfloat16)


def solution(mesh):
    in_specs = (
        P("req", "tp"),
        P("req", "tp"),
        P("req", "tp"),
        P("req", None, "tp"),
        P("req", None, "tp"),
        P("req", None),
        P("req"),
        P("req", None),
        P("req", None),
        P("tp", None),
        P(),
        P(),
        P("req", None),
        P("req", None, None, "tp"),
        P("req", "tp", None),
        P(None, None, "tp"),
        P("tp", None),
    )
    out_specs = P("req", "tp")
    return jax.shard_map(shards, mesh=mesh, in_specs=in_specs, out_specs=out_specs, check_vma=False)
```

```python
import math

import jax
import jax.numpy as jnp
from jax import lax
from jax.sharding import PartitionSpec as P

QH = 20
KVH = 4
HD = 128


EPSILON = 1e-06
NEGATIVE = -1e30


def rounded(values):
    return lax.optimization_barrier(values.astype(jnp.bfloat16)).astype(jnp.float32)


def ancestors(parents):
    tree_size = parents.shape[-1]
    position = jnp.arange(tree_size, dtype=jnp.int32)
    adjacency = (parents[..., :, None] == position[None, :]) | (
        position[:, None] == position[None, :]
    )
    closure = adjacency.astype(jnp.float32)
    for doubling in range(max(1, (tree_size - 1).bit_length())):
        closure = jnp.minimum(
            jnp.einsum("...ij,...jk->...ik", closure, closure, precision=lax.Precision.HIGHEST), 1.0
        )
    return closure > 0.5


def tree_attention(queries, cache_keys, cache_values, new_keys, new_values, lengths, allowed):
    scaling = 1.0 / math.sqrt(queries.shape[-1])
    cache_scores = (
        jnp.einsum("rtkgd,rckd->rkgtc", queries, cache_keys, preferred_element_type=jnp.float32)
        * scaling
    )
    tree_scores = (
        jnp.einsum("rtkgd,rskd->rkgts", queries, new_keys, preferred_element_type=jnp.float32)
        * scaling
    )
    live = jnp.arange(cache_keys.shape[1], dtype=jnp.int32)[None, :] < lengths[:, None]
    cache_scores = jnp.where(live[:, None, None, None, :], cache_scores, NEGATIVE)
    tree_scores = jnp.where(allowed[:, None, None, :, :], tree_scores, NEGATIVE)
    highest = jnp.maximum(jnp.max(cache_scores, axis=-1), jnp.max(tree_scores, axis=-1))[..., None]
    cache_exp = jnp.exp(cache_scores - highest)
    tree_exp = jnp.exp(tree_scores - highest)
    denominator = (jnp.sum(cache_exp, axis=-1) + jnp.sum(tree_exp, axis=-1))[..., None]
    cache_probs = (cache_exp / denominator).astype(jnp.bfloat16)
    tree_probs = (tree_exp / denominator).astype(jnp.bfloat16)
    mixed = jnp.einsum(
        "rkgtc,rckd->rtkgd", cache_probs, cache_values, preferred_element_type=jnp.float32
    )
    mixed = mixed + jnp.einsum(
        "rkgts,rskd->rtkgd", tree_probs, new_values, preferred_element_type=jnp.float32
    )
    return mixed.astype(jnp.bfloat16).reshape(queries.shape[0], queries.shape[1], -1)


def shards(
    queries,
    new_keys,
    new_values,
    key_pages,
    value_pages,
    page_table,
    cache_lengths,
    parents,
    residual,
    out_weight,
    norm_gain,
    router_weight,
    routes,
    expert_gate_up,
    expert_down,
    shared_gate_up,
    shared_down,
):
    groups = lax.axis_size("req")
    tp_count = lax.axis_size("tp")
    requests = parents.shape[0]
    tree_size = parents.shape[1]
    row_count = requests * tree_size
    kv_local = new_keys.shape[1] // HD
    head_ratio = QH // KVH
    model_width = residual.shape[1]
    part_width = model_width // tp_count
    pages_dev = key_pages.shape[0]
    local_pages = page_table - lax.axis_index("req") * pages_dev
    page_pick = (
        local_pages.reshape(-1)[:, None] == jnp.arange(pages_dev, dtype=jnp.int32)[None, :]
    ).astype(key_pages.dtype)
    cache_keys = jnp.dot(
        page_pick, key_pages.reshape(pages_dev, -1), preferred_element_type=jnp.float32
    ).astype(key_pages.dtype).reshape(requests, -1, kv_local, HD)
    cache_values = jnp.dot(
        page_pick, value_pages.reshape(pages_dev, -1), preferred_element_type=jnp.float32
    ).astype(value_pages.dtype).reshape(requests, -1, kv_local, HD)
    head_outputs = tree_attention(
        queries.reshape(requests, tree_size, kv_local, head_ratio, HD),
        cache_keys,
        cache_values,
        new_keys.reshape(requests, tree_size, kv_local, HD),
        new_values.reshape(requests, tree_size, kv_local, HD),
        cache_lengths,
        ancestors(parents),
    )
    attn_terms = jnp.dot(
        head_outputs.reshape(row_count, -1), out_weight, preferred_element_type=jnp.float32
    )
    column = lax.axis_index("tp") * part_width
    experts_local = expert_gate_up.shape[0]
    top_count = routes.shape[1]
    expert_count = experts_local * groups
    capacity = max(10 * requests, row_count * top_count * 5 // (4 * expert_count) + 1)
    capacity = -(-capacity // 16) * 16
    slot_count = expert_count * capacity

    flat_expert = routes.reshape(-1)
    expert_ids = jnp.arange(expert_count, dtype=jnp.int32)
    onehot = (flat_expert[:, None] == expert_ids[None, :]).astype(jnp.int32)
    earlier = jnp.cumsum(onehot, axis=0) - onehot
    rank = jnp.sum(earlier * onehot, axis=1)
    slot = (flat_expert * capacity + rank).reshape(row_count, top_count)
    slot_ids = jnp.arange(slot_count, dtype=jnp.int32)
    hit = slot[:, :, None] == slot_ids[None, None, :]

    attn_blocks = attn_terms.astype(jnp.bfloat16).reshape(row_count, tp_count, part_width)
    attn_blocks = lax.all_to_all(
        attn_blocks.transpose(1, 0, 2), "tp", split_axis=0, concat_axis=0, tiled=True
    )
    attn_part = jnp.sum(attn_blocks.astype(jnp.float32), axis=0)
    residual_part = lax.dynamic_slice_in_dim(residual, column, part_width, 1)
    hidden_part_bf = (residual_part.astype(jnp.float32) + attn_part).astype(jnp.bfloat16)
    hidden = lax.all_gather(hidden_part_bf, "tp", axis=1, tiled=True).astype(jnp.float32)
    rstd = lax.rsqrt(jnp.mean(hidden * hidden, axis=1, keepdims=True) + EPSILON)
    normed = hidden * rstd * norm_gain
    logits = jnp.dot(normed, router_weight, precision=lax.Precision.HIGHEST)
    normed_bf = normed.astype(jnp.bfloat16)
    hidden_part = hidden_part_bf.astype(jnp.float32)

    dispatch = jnp.any(hit, axis=1).astype(jnp.bfloat16)
    dispatch = dispatch.reshape(row_count, groups, experts_local, capacity)
    returns = []
    for expert in range(experts_local):
        outbox = jnp.einsum(
            "tgc,td->gcd", dispatch[:, :, expert], normed_bf, preferred_element_type=jnp.float32
        ).astype(jnp.bfloat16)
        arrived = lax.all_to_all(outbox, "req", split_axis=0, concat_axis=0, tiled=True)
        rows = arrived.reshape(groups * capacity, model_width)
        gate_up = jnp.einsum(
            "md,dcf->mcf", rows, expert_gate_up[expert], preferred_element_type=jnp.float32
        )
        act = (jax.nn.silu(gate_up[:, 0]) * gate_up[:, 1]).astype(jnp.bfloat16)
        partial_value = jnp.dot(act, expert_down[expert], preferred_element_type=jnp.float32)
        partial_bf = partial_value.astype(jnp.bfloat16)
        if expert < experts_local - 1:
            outputs = partial_bf.reshape(groups, capacity, model_width)
        else:
            outputs = lax.psum_scatter(
                partial_bf.reshape(-1, tp_count, part_width).transpose(1, 0, 2),
                "tp", scatter_dimension=0, tiled=True,
            ).reshape(groups, capacity, part_width)
        returns.append(lax.all_to_all(outputs, "req", split_axis=0, concat_axis=0, tiled=True))

    chosen = jnp.sum(
        jnp.where(routes[:, :, None] == expert_ids[None, None, :], logits[:, None, :], 0.0), axis=-1
    )
    gate_values = jax.nn.sigmoid(chosen)
    gate_values = gate_values / jnp.sum(gate_values, axis=1, keepdims=True)
    weights = jnp.sum(jnp.where(hit, gate_values[:, :, None], 0.0), axis=1)
    weights = weights.reshape(row_count, groups, experts_local, capacity)
    weights_hi = weights.astype(jnp.bfloat16)
    weights_lo = (weights - weights_hi.astype(jnp.float32)).astype(jnp.bfloat16)
    weights_split = jnp.stack([weights_hi, weights_lo])
    routed = jnp.zeros((row_count, model_width), jnp.float32)
    for expert in range(experts_local):
        both = jnp.einsum(
            "stgc,gcd->std", weights_split[:, :, :, expert], returns[expert],
            preferred_element_type=jnp.float32,
        )
        if expert < experts_local - 1:
            routed = routed + both[0] + both[1]
        else:
            routed_last = both[0] + both[1]

    shared_gu = jnp.einsum(
        "td,dcf->tcf", normed_bf, shared_gate_up, preferred_element_type=jnp.float32
    )
    shared_act = (jax.nn.silu(shared_gu[:, 0]) * shared_gu[:, 1]).astype(jnp.bfloat16)
    shared_terms = jnp.dot(shared_act, shared_down, preferred_element_type=jnp.float32)
    total = (shared_terms + routed).astype(jnp.bfloat16).reshape(row_count, tp_count, part_width)
    summed = lax.psum_scatter(total.transpose(1, 0, 2), "tp", scatter_dimension=0, tiled=True)
    summed = summed[0].astype(jnp.float32) + routed_last
    return (hidden_part + summed).astype(jnp.bfloat16)


def solution(mesh):
    in_specs = (
        P("req", "tp"),
        P("req", "tp"),
        P("req", "tp"),
        P("req", None, "tp"),
        P("req", None, "tp"),
        P("req", None),
        P("req"),
        P("req", None),
        P("req", None),
        P("tp", None),
        P(),
        P(),
        P("req", None),
        P("req", None, None, "tp"),
        P("req", "tp", None),
        P(None, None, "tp"),
        P("tp", None),
    )
    out_specs = P("req", "tp")
    return jax.shard_map(shards, mesh=mesh, in_specs=in_specs, out_specs=out_specs, check_vma=False)
```

```python
import math

import jax
import jax.numpy as jnp
from jax import lax
from jax.sharding import PartitionSpec as P

QH = 20
KVH = 4
HD = 128


EPSILON = 1e-06
NEGATIVE = -1e30


def rounded(values):
    return lax.optimization_barrier(values.astype(jnp.bfloat16)).astype(jnp.float32)


def ancestors(parents):
    tree_size = parents.shape[-1]
    position = jnp.arange(tree_size, dtype=jnp.int32)
    adjacency = (parents[..., :, None] == position[None, :]) | (
        position[:, None] == position[None, :]
    )
    closure = adjacency.astype(jnp.float32)
    for doubling in range(max(1, (tree_size - 1).bit_length())):
        closure = jnp.minimum(
            jnp.einsum("...ij,...jk->...ik", closure, closure, precision=lax.Precision.HIGHEST), 1.0
        )
    return closure > 0.5


def tree_attention(queries, cache_keys, cache_values, new_keys, new_values, lengths, allowed):
    scaling = 1.0 / math.sqrt(queries.shape[-1])
    cache_scores = (
        jnp.einsum("rtkgd,rckd->rkgtc", queries, cache_keys, preferred_element_type=jnp.float32)
        * scaling
    )
    tree_scores = (
        jnp.einsum("rtkgd,rskd->rkgts", queries, new_keys, preferred_element_type=jnp.float32)
        * scaling
    )
    live = jnp.arange(cache_keys.shape[1], dtype=jnp.int32)[None, :] < lengths[:, None]
    cache_scores = jnp.where(live[:, None, None, None, :], cache_scores, NEGATIVE)
    tree_scores = jnp.where(allowed[:, None, None, :, :], tree_scores, NEGATIVE)
    highest = jnp.maximum(jnp.max(cache_scores, axis=-1), jnp.max(tree_scores, axis=-1))[..., None]
    cache_exp = jnp.exp(cache_scores - highest)
    tree_exp = jnp.exp(tree_scores - highest)
    denominator = (jnp.sum(cache_exp, axis=-1) + jnp.sum(tree_exp, axis=-1))[..., None]
    cache_probs = (cache_exp / denominator).astype(jnp.bfloat16)
    tree_probs = (tree_exp / denominator).astype(jnp.bfloat16)
    mixed = jnp.einsum(
        "rkgtc,rckd->rtkgd", cache_probs, cache_values, preferred_element_type=jnp.float32
    )
    mixed = mixed + jnp.einsum(
        "rkgts,rskd->rtkgd", tree_probs, new_values, preferred_element_type=jnp.float32
    )
    return mixed.astype(jnp.bfloat16).reshape(queries.shape[0], queries.shape[1], -1)


def shards(
    queries,
    new_keys,
    new_values,
    key_pages,
    value_pages,
    page_table,
    cache_lengths,
    parents,
    residual,
    out_weight,
    norm_gain,
    router_weight,
    routes,
    expert_gate_up,
    expert_down,
    shared_gate_up,
    shared_down,
):
    groups = lax.axis_size("req")
    tp_count = lax.axis_size("tp")
    requests = parents.shape[0]
    tree_size = parents.shape[1]
    row_count = requests * tree_size
    kv_local = new_keys.shape[1] // HD
    head_ratio = QH // KVH
    model_width = residual.shape[1]
    part_width = model_width // tp_count
    pages_dev = key_pages.shape[0]
    local_pages = page_table - lax.axis_index("req") * pages_dev
    cache_keys = key_pages[local_pages].reshape(requests, -1, kv_local, HD)
    cache_values = value_pages[local_pages].reshape(requests, -1, kv_local, HD)
    head_outputs = tree_attention(
        queries.reshape(requests, tree_size, kv_local, head_ratio, HD),
        cache_keys,
        cache_values,
        new_keys.reshape(requests, tree_size, kv_local, HD),
        new_values.reshape(requests, tree_size, kv_local, HD),
        cache_lengths,
        ancestors(parents),
    )
    attn_terms = jnp.dot(
        head_outputs.reshape(row_count, -1), out_weight, preferred_element_type=jnp.float32
    )
    column = lax.axis_index("tp") * part_width
    experts_local = expert_gate_up.shape[0]
    top_count = routes.shape[1]
    expert_count = experts_local * groups
    capacity = max(10 * requests, row_count * top_count * 5 // (4 * expert_count) + 1)
    capacity = -(-capacity // 16) * 16
    slot_count = expert_count * capacity

    flat_expert = routes.reshape(-1)
    expert_ids = jnp.arange(expert_count, dtype=jnp.int32)
    onehot = (flat_expert[:, None] == expert_ids[None, :]).astype(jnp.int32)
    earlier = jnp.cumsum(onehot, axis=0) - onehot
    rank = jnp.sum(earlier * onehot, axis=1)
    slot = (flat_expert * capacity + rank).reshape(row_count, top_count)
    slot_ids = jnp.arange(slot_count, dtype=jnp.int32)
    hit = slot[:, :, None] == slot_ids[None, None, :]

    attn_blocks = attn_terms.astype(jnp.bfloat16).reshape(row_count, tp_count, part_width)
    attn_blocks = lax.all_to_all(
        attn_blocks.transpose(1, 0, 2), "tp", split_axis=0, concat_axis=0, tiled=True
    )
    attn_part = jnp.sum(attn_blocks.astype(jnp.float32), axis=0)
    residual_part = lax.dynamic_slice_in_dim(residual, column, part_width, 1)
    hidden_part_bf = (residual_part.astype(jnp.float32) + attn_part).astype(jnp.bfloat16)
    hidden_bf = lax.all_gather(hidden_part_bf[None], "tp", axis=0, tiled=True)
    hidden = hidden_bf.transpose(1, 0, 2).reshape(row_count, model_width).astype(jnp.float32)
    rstd = lax.rsqrt(jnp.mean(hidden * hidden, axis=1, keepdims=True) + EPSILON)
    normed = hidden * rstd * norm_gain
    logits = jnp.dot(normed, router_weight, precision=lax.Precision.HIGHEST)
    normed_bf = normed.astype(jnp.bfloat16)
    hidden_part = hidden_part_bf.astype(jnp.float32)

    dispatch = jnp.any(hit, axis=1).astype(jnp.bfloat16)
    dispatch = dispatch.reshape(row_count, groups, experts_local, capacity)
    returns = []
    for expert in range(experts_local):
        outbox = jnp.einsum(
            "tgc,td->gcd", dispatch[:, :, expert], normed_bf, preferred_element_type=jnp.float32
        ).astype(jnp.bfloat16)
        arrived = lax.all_to_all(outbox, "req", split_axis=0, concat_axis=0, tiled=True)
        rows = arrived.reshape(groups * capacity, model_width)
        hidden_units = expert_gate_up.shape[-1]
        gate_up = jnp.dot(
            rows, expert_gate_up[expert].reshape(model_width, 2 * hidden_units),
            preferred_element_type=jnp.float32,
        )
        act = (
            jax.nn.silu(gate_up[:, :hidden_units]) * gate_up[:, hidden_units:]
        ).astype(jnp.bfloat16)
        partial_value = jnp.dot(act, expert_down[expert], preferred_element_type=jnp.float32)
        partial_bf = partial_value.astype(jnp.bfloat16)
        if expert < experts_local - 1:
            outputs = partial_bf.reshape(groups, capacity, model_width)
        else:
            outputs = lax.psum_scatter(
                partial_bf.reshape(-1, tp_count, part_width).transpose(1, 0, 2),
                "tp", scatter_dimension=0, tiled=True,
            ).reshape(groups, capacity, part_width)
        returns.append(lax.all_to_all(outputs, "req", split_axis=0, concat_axis=0, tiled=True))

    chosen = jnp.sum(
        jnp.where(routes[:, :, None] == expert_ids[None, None, :], logits[:, None, :], 0.0), axis=-1
    )
    gate_values = jax.nn.sigmoid(chosen)
    gate_values = gate_values / jnp.sum(gate_values, axis=1, keepdims=True)
    weights = jnp.sum(jnp.where(hit, gate_values[:, :, None], 0.0), axis=1)
    weights = weights.reshape(row_count, groups, experts_local, capacity)
    weights_hi = weights.astype(jnp.bfloat16)
    weights_lo = (weights - weights_hi.astype(jnp.float32)).astype(jnp.bfloat16)
    weights_split = jnp.stack([weights_hi, weights_lo])
    routed = jnp.zeros((row_count, model_width), jnp.float32)
    for expert in range(experts_local):
        both = jnp.einsum(
            "stgc,gcd->std", weights_split[:, :, :, expert], returns[expert],
            preferred_element_type=jnp.float32,
        )
        if expert < experts_local - 1:
            routed = routed + both[0] + both[1]
        else:
            routed_last = both[0] + both[1]

    shared_units = shared_gate_up.shape[-1]
    shared_gu = jnp.dot(
        normed_bf, shared_gate_up.reshape(model_width, 2 * shared_units),
        preferred_element_type=jnp.float32,
    )
    shared_act = (
        jax.nn.silu(shared_gu[:, :shared_units]) * shared_gu[:, shared_units:]
    ).astype(jnp.bfloat16)
    shared_terms = jnp.dot(shared_act, shared_down, preferred_element_type=jnp.float32)
    total = (shared_terms + routed).astype(jnp.bfloat16).reshape(row_count, tp_count, part_width)
    summed = lax.psum_scatter(total.transpose(1, 0, 2), "tp", scatter_dimension=0, tiled=True)
    summed = summed[0].astype(jnp.float32) + routed_last
    return (hidden_part + summed).astype(jnp.bfloat16)


def solution(mesh):
    in_specs = (
        P("req", "tp"),
        P("req", "tp"),
        P("req", "tp"),
        P("req", None, "tp"),
        P("req", None, "tp"),
        P("req", None),
        P("req"),
        P("req", None),
        P("req", None),
        P("tp", None),
        P(),
        P(),
        P("req", None),
        P("req", None, None, "tp"),
        P("req", "tp", None),
        P(None, None, "tp"),
        P("tp", None),
    )
    out_specs = P("req", "tp")
    return jax.shard_map(shards, mesh=mesh, in_specs=in_specs, out_specs=out_specs, check_vma=False)
```

```python
import math

import jax
import jax.numpy as jnp
from jax import lax
from jax.sharding import PartitionSpec as P

QH = 20
KVH = 4
HD = 128


EPSILON = 1e-06
NEGATIVE = -1e30


def rounded(values):
    return lax.optimization_barrier(values.astype(jnp.bfloat16)).astype(jnp.float32)


def ancestors(parents):
    tree_size = parents.shape[-1]
    position = jnp.arange(tree_size, dtype=jnp.int32)
    adjacency = (parents[..., :, None] == position[None, :]) | (
        position[:, None] == position[None, :]
    )
    closure = adjacency.astype(jnp.float32)
    for doubling in range(max(1, (tree_size - 1).bit_length())):
        closure = jnp.minimum(
            jnp.einsum("...ij,...jk->...ik", closure, closure, precision=lax.Precision.HIGHEST), 1.0
        )
    return closure > 0.5


def tree_attention(queries, cache_keys, cache_values, new_keys, new_values, lengths, allowed):
    scaling = 1.0 / math.sqrt(queries.shape[-1])
    cache_scores = (
        jnp.einsum("rtkgd,rckd->rkgtc", queries, cache_keys, preferred_element_type=jnp.float32)
        * scaling
    )
    tree_scores = (
        jnp.einsum("rtkgd,rskd->rkgts", queries, new_keys, preferred_element_type=jnp.float32)
        * scaling
    )
    live = jnp.arange(cache_keys.shape[1], dtype=jnp.int32)[None, :] < lengths[:, None]
    cache_scores = jnp.where(live[:, None, None, None, :], cache_scores, NEGATIVE)
    tree_scores = jnp.where(allowed[:, None, None, :, :], tree_scores, NEGATIVE)
    highest = jnp.maximum(jnp.max(cache_scores, axis=-1), jnp.max(tree_scores, axis=-1))[..., None]
    cache_exp = jnp.exp(cache_scores - highest)
    tree_exp = jnp.exp(tree_scores - highest)
    denominator = (jnp.sum(cache_exp, axis=-1) + jnp.sum(tree_exp, axis=-1))[..., None]
    cache_probs = (cache_exp / denominator).astype(jnp.bfloat16)
    tree_probs = (tree_exp / denominator).astype(jnp.bfloat16)
    mixed = jnp.einsum(
        "rkgtc,rckd->rtkgd", cache_probs, cache_values, preferred_element_type=jnp.float32
    )
    mixed = mixed + jnp.einsum(
        "rkgts,rskd->rtkgd", tree_probs, new_values, preferred_element_type=jnp.float32
    )
    return mixed.astype(jnp.bfloat16).reshape(queries.shape[0], queries.shape[1], -1)


def shards(
    queries,
    new_keys,
    new_values,
    key_pages,
    value_pages,
    page_table,
    cache_lengths,
    parents,
    residual,
    out_weight,
    norm_gain,
    router_weight,
    routes,
    expert_gate_up,
    expert_down,
    shared_gate_up,
    shared_down,
):
    groups = lax.axis_size("req")
    tp_count = lax.axis_size("tp")
    requests = parents.shape[0]
    tree_size = parents.shape[1]
    row_count = requests * tree_size
    kv_local = new_keys.shape[1] // HD
    head_ratio = QH // KVH
    model_width = residual.shape[1]
    part_width = model_width // tp_count
    pages_dev = key_pages.shape[0]
    local_pages = page_table - lax.axis_index("req") * pages_dev
    cache_keys = key_pages[local_pages].reshape(requests, -1, kv_local, HD)
    cache_values = value_pages[local_pages].reshape(requests, -1, kv_local, HD)
    head_outputs = tree_attention(
        queries.reshape(requests, tree_size, kv_local, head_ratio, HD),
        cache_keys,
        cache_values,
        new_keys.reshape(requests, tree_size, kv_local, HD),
        new_values.reshape(requests, tree_size, kv_local, HD),
        cache_lengths,
        ancestors(parents),
    )
    attn_terms = jnp.dot(
        head_outputs.reshape(row_count, -1), out_weight, preferred_element_type=jnp.float32
    )
    column = lax.axis_index("tp") * part_width
    experts_local = expert_gate_up.shape[0]
    top_count = routes.shape[1]
    expert_count = experts_local * groups
    capacity = max(10 * requests, row_count * top_count * 5 // (4 * expert_count) + 1)
    capacity = -(-capacity // 16) * 16
    slot_count = expert_count * capacity

    flat_expert = routes.reshape(-1)
    expert_ids = jnp.arange(expert_count, dtype=jnp.int32)
    onehot = (flat_expert[:, None] == expert_ids[None, :]).astype(jnp.int32)
    earlier = jnp.cumsum(onehot, axis=0) - onehot
    rank = jnp.sum(earlier * onehot, axis=1)
    slot = (flat_expert * capacity + rank).reshape(row_count, top_count)
    slot_ids = jnp.arange(slot_count, dtype=jnp.int32)
    hit = slot[:, :, None] == slot_ids[None, None, :]

    attn_blocks = attn_terms.astype(jnp.bfloat16).reshape(row_count, tp_count, part_width)
    attn_blocks = lax.all_to_all(
        attn_blocks.transpose(1, 0, 2), "tp", split_axis=0, concat_axis=0, tiled=True
    )
    attn_part = jnp.sum(attn_blocks.astype(jnp.float32), axis=0)
    residual_part = lax.dynamic_slice_in_dim(residual, column, part_width, 1)
    hidden_part_bf = (residual_part.astype(jnp.float32) + attn_part).astype(jnp.bfloat16)
    hidden_bf = lax.all_gather(hidden_part_bf[None], "tp", axis=0, tiled=True)
    hidden = hidden_bf.transpose(1, 0, 2).reshape(row_count, model_width).astype(jnp.float32)
    rstd = lax.rsqrt(jnp.mean(hidden * hidden, axis=1, keepdims=True) + EPSILON)
    normed = hidden * rstd * norm_gain
    logits = jnp.dot(normed, router_weight, precision=lax.Precision.HIGHEST)
    normed_bf = normed.astype(jnp.bfloat16)
    hidden_part = hidden_part_bf.astype(jnp.float32)

    dispatch = jnp.any(hit, axis=1).astype(jnp.bfloat16)
    dispatch = dispatch.reshape(row_count, groups, experts_local, capacity)
    returns = []
    for expert in range(experts_local):
        outbox = jnp.einsum(
            "tgc,td->gcd", dispatch[:, :, expert], normed_bf, preferred_element_type=jnp.float32
        ).astype(jnp.bfloat16)
        arrived = lax.all_to_all(outbox, "req", split_axis=0, concat_axis=0, tiled=True)
        rows = arrived.reshape(groups * capacity, model_width)
        gate = jnp.dot(rows, expert_gate_up[expert, :, 0], preferred_element_type=jnp.float32)
        up = jnp.dot(rows, expert_gate_up[expert, :, 1], preferred_element_type=jnp.float32)
        act = (jax.nn.silu(gate) * up).astype(jnp.bfloat16)
        partial_value = jnp.dot(act, expert_down[expert], preferred_element_type=jnp.float32)
        partial_bf = partial_value.astype(jnp.bfloat16)
        if expert < experts_local - 1:
            outputs = partial_bf.reshape(groups, capacity, model_width)
        else:
            outputs = lax.psum_scatter(
                partial_bf.reshape(-1, tp_count, part_width).transpose(1, 0, 2),
                "tp", scatter_dimension=0, tiled=True,
            ).reshape(groups, capacity, part_width)
        returns.append(lax.all_to_all(outputs, "req", split_axis=0, concat_axis=0, tiled=True))

    chosen = jnp.sum(
        jnp.where(routes[:, :, None] == expert_ids[None, None, :], logits[:, None, :], 0.0), axis=-1
    )
    gate_values = jax.nn.sigmoid(chosen)
    gate_values = gate_values / jnp.sum(gate_values, axis=1, keepdims=True)
    weights = jnp.sum(jnp.where(hit, gate_values[:, :, None], 0.0), axis=1)
    weights = weights.reshape(row_count, groups, experts_local, capacity)
    weights_hi = weights.astype(jnp.bfloat16)
    weights_lo = (weights - weights_hi.astype(jnp.float32)).astype(jnp.bfloat16)
    weights_split = jnp.stack([weights_hi, weights_lo])
    routed = jnp.zeros((row_count, model_width), jnp.float32)
    for expert in range(experts_local):
        both = jnp.einsum(
            "stgc,gcd->std", weights_split[:, :, :, expert], returns[expert],
            preferred_element_type=jnp.float32,
        )
        if expert < experts_local - 1:
            routed = routed + both[0] + both[1]
        else:
            routed_last = both[0] + both[1]

    shared_gu = jnp.einsum(
        "td,dcf->tcf", normed_bf, shared_gate_up, preferred_element_type=jnp.float32
    )
    shared_act = (jax.nn.silu(shared_gu[:, 0]) * shared_gu[:, 1]).astype(jnp.bfloat16)
    shared_terms = jnp.dot(shared_act, shared_down, preferred_element_type=jnp.float32)
    total = (shared_terms + routed).astype(jnp.bfloat16).reshape(row_count, tp_count, part_width)
    summed = lax.psum_scatter(total.transpose(1, 0, 2), "tp", scatter_dimension=0, tiled=True)
    summed = summed[0].astype(jnp.float32) + routed_last
    return (hidden_part + summed).astype(jnp.bfloat16)


def solution(mesh):
    in_specs = (
        P("req", "tp"),
        P("req", "tp"),
        P("req", "tp"),
        P("req", None, "tp"),
        P("req", None, "tp"),
        P("req", None),
        P("req"),
        P("req", None),
        P("req", None),
        P("tp", None),
        P(),
        P(),
        P("req", None),
        P("req", None, None, "tp"),
        P("req", "tp", None),
        P(None, None, "tp"),
        P("tp", None),
    )
    out_specs = P("req", "tp")
    return jax.shard_map(shards, mesh=mesh, in_specs=in_specs, out_specs=out_specs, check_vma=False)
```

```python
import math

import jax
import jax.numpy as jnp
from jax import lax
from jax.sharding import PartitionSpec as P

QH = 20
KVH = 4
HD = 128


EPSILON = 1e-06
NEGATIVE = -1e30


def rounded(values):
    return lax.optimization_barrier(values.astype(jnp.bfloat16)).astype(jnp.float32)


def ancestors(parents):
    tree_size = parents.shape[-1]
    position = jnp.arange(tree_size, dtype=jnp.int32)
    adjacency = (parents[..., :, None] == position[None, :]) | (
        position[:, None] == position[None, :]
    )
    closure = adjacency.astype(jnp.float32)
    for doubling in range(max(1, (tree_size - 1).bit_length())):
        closure = jnp.minimum(
            jnp.einsum("...ij,...jk->...ik", closure, closure, precision=lax.Precision.HIGHEST), 1.0
        )
    return closure > 0.5


def tree_attention(queries, cache_keys, cache_values, new_keys, new_values, lengths, allowed):
    scaling = 1.0 / math.sqrt(queries.shape[-1])
    cache_scores = (
        jnp.einsum("rtkgd,rckd->rkgtc", queries, cache_keys, preferred_element_type=jnp.float32)
        * scaling
    )
    tree_scores = (
        jnp.einsum("rtkgd,rskd->rkgts", queries, new_keys, preferred_element_type=jnp.float32)
        * scaling
    )
    live = jnp.arange(cache_keys.shape[1], dtype=jnp.int32)[None, :] < lengths[:, None]
    cache_scores = jnp.where(live[:, None, None, None, :], cache_scores, NEGATIVE)
    tree_scores = jnp.where(allowed[:, None, None, :, :], tree_scores, NEGATIVE)
    highest = jnp.maximum(jnp.max(cache_scores, axis=-1), jnp.max(tree_scores, axis=-1))[..., None]
    cache_exp = jnp.exp(cache_scores - highest)
    tree_exp = jnp.exp(tree_scores - highest)
    denominator = (jnp.sum(cache_exp, axis=-1) + jnp.sum(tree_exp, axis=-1))[..., None]
    cache_probs = (cache_exp / denominator).astype(jnp.bfloat16)
    tree_probs = (tree_exp / denominator).astype(jnp.bfloat16)
    mixed = jnp.einsum(
        "rkgtc,rckd->rtkgd", cache_probs, cache_values, preferred_element_type=jnp.float32
    )
    mixed = mixed + jnp.einsum(
        "rkgts,rskd->rtkgd", tree_probs, new_values, preferred_element_type=jnp.float32
    )
    return mixed.astype(jnp.bfloat16).reshape(queries.shape[0], queries.shape[1], -1)


def shards(
    queries,
    new_keys,
    new_values,
    key_pages,
    value_pages,
    page_table,
    cache_lengths,
    parents,
    residual,
    out_weight,
    norm_gain,
    router_weight,
    routes,
    expert_gate_up,
    expert_down,
    shared_gate_up,
    shared_down,
):
    groups = lax.axis_size("req")
    tp_count = lax.axis_size("tp")
    requests = parents.shape[0]
    tree_size = parents.shape[1]
    row_count = requests * tree_size
    kv_local = new_keys.shape[1] // HD
    head_ratio = QH // KVH
    model_width = residual.shape[1]
    part_width = model_width // tp_count
    pages_dev = key_pages.shape[0]
    local_pages = page_table - lax.axis_index("req") * pages_dev
    cache_keys = key_pages[local_pages].reshape(requests, -1, kv_local, HD)
    cache_values = value_pages[local_pages].reshape(requests, -1, kv_local, HD)
    head_outputs = tree_attention(
        queries.reshape(requests, tree_size, kv_local, head_ratio, HD),
        cache_keys,
        cache_values,
        new_keys.reshape(requests, tree_size, kv_local, HD),
        new_values.reshape(requests, tree_size, kv_local, HD),
        cache_lengths,
        ancestors(parents),
    )
    attn_terms = jnp.dot(
        head_outputs.reshape(row_count, -1), out_weight, preferred_element_type=jnp.float32
    )
    column = lax.axis_index("tp") * part_width
    experts_local = expert_gate_up.shape[0]
    top_count = routes.shape[1]
    expert_count = experts_local * groups
    capacity = max(10 * requests, row_count * top_count * 5 // (4 * expert_count) + 1)
    capacity = -(-capacity // 16) * 16
    slot_count = expert_count * capacity

    flat_expert = routes.reshape(-1)
    expert_ids = jnp.arange(expert_count, dtype=jnp.int32)
    onehot = (flat_expert[:, None] == expert_ids[None, :]).astype(jnp.int32)
    earlier = jnp.cumsum(onehot, axis=0) - onehot
    rank = jnp.sum(earlier * onehot, axis=1)
    slot = (flat_expert * capacity + rank).reshape(row_count, top_count)
    slot_ids = jnp.arange(slot_count, dtype=jnp.int32)
    hit = slot[:, :, None] == slot_ids[None, None, :]

    attn_blocks = attn_terms.astype(jnp.bfloat16).reshape(row_count, tp_count, part_width)
    attn_blocks = lax.all_to_all(
        attn_blocks.transpose(1, 0, 2), "tp", split_axis=0, concat_axis=0, tiled=True
    )
    attn_part = jnp.sum(attn_blocks.astype(jnp.float32), axis=0)
    residual_part = lax.dynamic_slice_in_dim(residual, column, part_width, 1)
    hidden_part_bf = (residual_part.astype(jnp.float32) + attn_part).astype(jnp.bfloat16)
    hidden_bf = lax.all_gather(hidden_part_bf[None], "tp", axis=0, tiled=True)
    hidden = hidden_bf.transpose(1, 0, 2).reshape(row_count, model_width).astype(jnp.float32)
    rstd = lax.rsqrt(jnp.mean(hidden * hidden, axis=1, keepdims=True) + EPSILON)
    normed = hidden * rstd * norm_gain
    logits = jnp.dot(normed, router_weight, precision=lax.Precision.HIGHEST)
    normed_bf = normed.astype(jnp.bfloat16)
    hidden_part = hidden_part_bf.astype(jnp.float32)

    dispatch = jnp.any(hit, axis=1).astype(jnp.bfloat16)
    dispatch = dispatch.reshape(row_count, groups, experts_local, capacity)
    returns = []
    for expert in range(experts_local):
        outbox = jnp.einsum(
            "tgc,td->gcd", dispatch[:, :, expert], normed_bf, preferred_element_type=jnp.float32
        ).astype(jnp.bfloat16)
        arrived = lax.all_to_all(outbox, "req", split_axis=0, concat_axis=0, tiled=True)
        rows = arrived.reshape(groups * capacity, model_width)
        gate_up = jnp.einsum(
            "md,dcf->mcf", rows, expert_gate_up[expert], preferred_element_type=jnp.float32
        )
        act = (jax.nn.silu(gate_up[:, 0]) * gate_up[:, 1]).astype(jnp.bfloat16)
        partial_value = jnp.dot(act, expert_down[expert], preferred_element_type=jnp.float32)
        partial_bf = partial_value.astype(jnp.bfloat16)
        if expert < experts_local - 1:
            outputs = partial_bf.reshape(groups, capacity, model_width)
        else:
            outputs = lax.psum_scatter(
                partial_bf.reshape(-1, tp_count, part_width).transpose(1, 0, 2),
                "tp", scatter_dimension=0, tiled=True,
            ).reshape(groups, capacity, part_width)
        returns.append(lax.all_to_all(outputs, "req", split_axis=0, concat_axis=0, tiled=True))

    chosen = jnp.sum(
        jnp.where(routes[:, :, None] == expert_ids[None, None, :], logits[:, None, :], 0.0), axis=-1
    )
    gate_values = jax.nn.sigmoid(chosen)
    gate_values = gate_values / jnp.sum(gate_values, axis=1, keepdims=True)
    weights = jnp.sum(jnp.where(hit, gate_values[:, :, None], 0.0), axis=1)
    weights = weights.reshape(row_count, groups, experts_local, capacity)
    weights_bf = weights.astype(jnp.bfloat16)
    routed = jnp.zeros((row_count, model_width), jnp.float32)
    for expert in range(experts_local):
        both = jnp.einsum(
            "tgc,gcd->td", weights_bf[:, :, expert], returns[expert],
            preferred_element_type=jnp.float32,
        )
        if expert < experts_local - 1:
            routed = routed + both
        else:
            routed_last = both

    shared_gu = jnp.einsum(
        "td,dcf->tcf", normed_bf, shared_gate_up, preferred_element_type=jnp.float32
    )
    shared_act = (jax.nn.silu(shared_gu[:, 0]) * shared_gu[:, 1]).astype(jnp.bfloat16)
    shared_terms = jnp.dot(shared_act, shared_down, preferred_element_type=jnp.float32)
    total = (shared_terms + routed).astype(jnp.bfloat16).reshape(row_count, tp_count, part_width)
    summed = lax.psum_scatter(total.transpose(1, 0, 2), "tp", scatter_dimension=0, tiled=True)
    summed = summed[0].astype(jnp.float32) + routed_last
    return (hidden_part + summed).astype(jnp.bfloat16)


def solution(mesh):
    in_specs = (
        P("req", "tp"),
        P("req", "tp"),
        P("req", "tp"),
        P("req", None, "tp"),
        P("req", None, "tp"),
        P("req", None),
        P("req"),
        P("req", None),
        P("req", None),
        P("tp", None),
        P(),
        P(),
        P("req", None),
        P("req", None, None, "tp"),
        P("req", "tp", None),
        P(None, None, "tp"),
        P("tp", None),
    )
    out_specs = P("req", "tp")
    return jax.shard_map(shards, mesh=mesh, in_specs=in_specs, out_specs=out_specs, check_vma=False)
```

```python
import math

import jax
import jax.numpy as jnp
from jax import lax
from jax.sharding import PartitionSpec as P

QH = 20
KVH = 4
HD = 128


EPSILON = 1e-06
NEGATIVE = -1e30


def rounded(values):
    return lax.optimization_barrier(values.astype(jnp.bfloat16)).astype(jnp.float32)


def ancestors(parents):
    tree_size = parents.shape[-1]
    position = jnp.arange(tree_size, dtype=jnp.int32)
    adjacency = (parents[..., :, None] == position[None, :]) | (
        position[:, None] == position[None, :]
    )
    closure = adjacency.astype(jnp.float32)
    for doubling in range(max(1, (tree_size - 1).bit_length())):
        closure = jnp.minimum(
            jnp.einsum("...ij,...jk->...ik", closure, closure, precision=lax.Precision.HIGHEST), 1.0
        )
    return closure > 0.5


def tree_attention(queries, cache_keys, cache_values, new_keys, new_values, lengths, allowed):
    scaling = 1.0 / math.sqrt(queries.shape[-1])
    cache_scores = (
        jnp.einsum("rtkgd,rckd->rkgtc", queries, cache_keys, preferred_element_type=jnp.float32)
        * scaling
    )
    tree_scores = (
        jnp.einsum("rtkgd,rskd->rkgts", queries, new_keys, preferred_element_type=jnp.float32)
        * scaling
    )
    live = jnp.arange(cache_keys.shape[1], dtype=jnp.int32)[None, :] < lengths[:, None]
    cache_scores = jnp.where(live[:, None, None, None, :], cache_scores, NEGATIVE)
    tree_scores = jnp.where(allowed[:, None, None, :, :], tree_scores, NEGATIVE)
    highest = jnp.maximum(jnp.max(cache_scores, axis=-1), jnp.max(tree_scores, axis=-1))[..., None]
    cache_exp = jnp.exp(cache_scores - highest)
    tree_exp = jnp.exp(tree_scores - highest)
    denominator = (jnp.sum(cache_exp, axis=-1) + jnp.sum(tree_exp, axis=-1))[..., None]
    cache_probs = (cache_exp / denominator).astype(jnp.bfloat16)
    tree_probs = (tree_exp / denominator).astype(jnp.bfloat16)
    mixed = jnp.einsum(
        "rkgtc,rckd->rtkgd", cache_probs, cache_values, preferred_element_type=jnp.float32
    )
    mixed = mixed + jnp.einsum(
        "rkgts,rskd->rtkgd", tree_probs, new_values, preferred_element_type=jnp.float32
    )
    return mixed.astype(jnp.bfloat16).reshape(queries.shape[0], queries.shape[1], -1)


def shards(
    queries,
    new_keys,
    new_values,
    key_pages,
    value_pages,
    page_table,
    cache_lengths,
    parents,
    residual,
    out_weight,
    norm_gain,
    router_weight,
    routes,
    expert_gate_up,
    expert_down,
    shared_gate_up,
    shared_down,
):
    groups = lax.axis_size("req")
    tp_count = lax.axis_size("tp")
    requests = parents.shape[0]
    tree_size = parents.shape[1]
    row_count = requests * tree_size
    kv_local = new_keys.shape[1] // HD
    head_ratio = QH // KVH
    model_width = residual.shape[1]
    part_width = model_width // tp_count
    pages_dev = key_pages.shape[0]
    local_pages = page_table - lax.axis_index("req") * pages_dev
    cache_keys = key_pages[local_pages].reshape(requests, -1, kv_local, HD)
    cache_values = value_pages[local_pages].reshape(requests, -1, kv_local, HD)
    head_outputs = tree_attention(
        queries.reshape(requests, tree_size, kv_local, head_ratio, HD),
        cache_keys,
        cache_values,
        new_keys.reshape(requests, tree_size, kv_local, HD),
        new_values.reshape(requests, tree_size, kv_local, HD),
        cache_lengths,
        ancestors(parents),
    )
    attn_terms = jnp.dot(
        head_outputs.reshape(row_count, -1), out_weight, preferred_element_type=jnp.float32
    )
    column = lax.axis_index("tp") * part_width
    experts_local = expert_gate_up.shape[0]
    top_count = routes.shape[1]
    expert_count = experts_local * groups
    capacity = max(10 * requests, row_count * top_count * 5 // (4 * expert_count) + 1)
    capacity = -(-capacity // 16) * 16
    slot_count = expert_count * capacity

    flat_expert = routes.reshape(-1)
    expert_ids = jnp.arange(expert_count, dtype=jnp.int32)
    onehot = (flat_expert[:, None] == expert_ids[None, :]).astype(jnp.int32)
    earlier = jnp.cumsum(onehot, axis=0) - onehot
    rank = jnp.sum(earlier * onehot, axis=1)
    slot = (flat_expert * capacity + rank).reshape(row_count, top_count)
    slot_ids = jnp.arange(slot_count, dtype=jnp.int32)
    hit = slot[:, :, None] == slot_ids[None, None, :]

    attn_blocks = attn_terms.astype(jnp.bfloat16).reshape(row_count, tp_count, part_width)
    attn_blocks = lax.all_to_all(
        attn_blocks.transpose(1, 0, 2), "tp", split_axis=0, concat_axis=0, tiled=True
    )
    attn_part = jnp.sum(attn_blocks.astype(jnp.float32), axis=0)
    residual_part = lax.dynamic_slice_in_dim(residual, column, part_width, 1)
    hidden_part_bf = (residual_part.astype(jnp.float32) + attn_part).astype(jnp.bfloat16)
    hidden = lax.all_gather(hidden_part_bf, "tp", axis=1, tiled=True).astype(jnp.float32)
    rstd = lax.rsqrt(jnp.mean(hidden * hidden, axis=1, keepdims=True) + EPSILON)
    normed = hidden * rstd * norm_gain
    logits = jnp.dot(normed, router_weight, precision=lax.Precision.HIGHEST)
    normed_bf = normed.astype(jnp.bfloat16)
    hidden_part = hidden_part_bf.astype(jnp.float32)

    dispatch = jnp.any(hit, axis=1).astype(jnp.bfloat16)
    dispatch = dispatch.reshape(row_count, groups, experts_local, capacity)
    returns = []
    for expert in range(experts_local):
        outbox = jnp.einsum(
            "tgc,td->gcd", dispatch[:, :, expert], normed_bf, preferred_element_type=jnp.float32
        ).astype(jnp.bfloat16)
        arrived = lax.all_to_all(outbox, "req", split_axis=0, concat_axis=0, tiled=True)
        rows = arrived.reshape(groups * capacity, model_width)
        gate_up = jnp.einsum(
            "md,dcf->mcf", rows, expert_gate_up[expert], preferred_element_type=jnp.float32
        )
        act = (jax.nn.silu(gate_up[:, 0]) * gate_up[:, 1]).astype(jnp.bfloat16)
        partial_value = jnp.dot(act, expert_down[expert], preferred_element_type=jnp.float32)
        partial_bf = partial_value.astype(jnp.bfloat16)
        if expert < experts_local - 1:
            outputs = partial_bf.reshape(groups, capacity, model_width)
        else:
            outputs = lax.psum_scatter(
                partial_bf.reshape(-1, tp_count, part_width).transpose(1, 0, 2),
                "tp", scatter_dimension=0, tiled=True,
            ).reshape(groups, capacity, part_width)
        returns.append(lax.all_to_all(outputs, "req", split_axis=0, concat_axis=0, tiled=True))

    chosen = jnp.sum(
        jnp.where(routes[:, :, None] == expert_ids[None, None, :], logits[:, None, :], 0.0), axis=-1
    )
    gate_values = jax.nn.sigmoid(chosen)
    gate_values = gate_values / jnp.sum(gate_values, axis=1, keepdims=True)
    weights = jnp.sum(jnp.where(hit, gate_values[:, :, None], 0.0), axis=1)
    weights = weights.reshape(row_count, groups, experts_local, capacity)
    weights_bf = weights.astype(jnp.bfloat16)
    routed = jnp.zeros((row_count, model_width), jnp.float32)
    for expert in range(experts_local):
        both = jnp.einsum(
            "tgc,gcd->td", weights_bf[:, :, expert], returns[expert],
            preferred_element_type=jnp.float32,
        )
        if expert < experts_local - 1:
            routed = routed + both
        else:
            routed_last = both

    shared_gu = jnp.einsum(
        "td,dcf->tcf", normed_bf, shared_gate_up, preferred_element_type=jnp.float32
    )
    shared_act = (jax.nn.silu(shared_gu[:, 0]) * shared_gu[:, 1]).astype(jnp.bfloat16)
    shared_terms = jnp.dot(shared_act, shared_down, preferred_element_type=jnp.float32)
    total = (shared_terms + routed).astype(jnp.bfloat16).reshape(row_count, tp_count, part_width)
    summed = lax.psum_scatter(total.transpose(1, 0, 2), "tp", scatter_dimension=0, tiled=True)
    summed = summed[0].astype(jnp.float32) + routed_last
    return (hidden_part + summed).astype(jnp.bfloat16)


def solution(mesh):
    in_specs = (
        P("req", "tp"),
        P("req", "tp"),
        P("req", "tp"),
        P("req", None, "tp"),
        P("req", None, "tp"),
        P("req", None),
        P("req"),
        P("req", None),
        P("req", None),
        P("tp", None),
        P(),
        P(),
        P("req", None),
        P("req", None, None, "tp"),
        P("req", "tp", None),
        P(None, None, "tp"),
        P("tp", None),
    )
    out_specs = P("req", "tp")
    return jax.shard_map(shards, mesh=mesh, in_specs=in_specs, out_specs=out_specs, check_vma=False)
```

```python
import math

import jax
import jax.numpy as jnp
from jax import lax
from jax.sharding import PartitionSpec as P

QH = 20
KVH = 4
HD = 128


EPSILON = 1e-06
NEGATIVE = -1e30


def rounded(values):
    return lax.optimization_barrier(values.astype(jnp.bfloat16)).astype(jnp.float32)


def ancestors(parents):
    tree_size = parents.shape[-1]
    position = jnp.arange(tree_size, dtype=jnp.int32)
    adjacency = (parents[..., :, None] == position[None, :]) | (
        position[:, None] == position[None, :]
    )
    closure = adjacency.astype(jnp.float32)
    for doubling in range(max(1, (tree_size - 1).bit_length())):
        closure = jnp.minimum(
            jnp.einsum("...ij,...jk->...ik", closure, closure, precision=lax.Precision.HIGHEST), 1.0
        )
    return closure > 0.5


def tree_attention(queries, cache_keys, cache_values, new_keys, new_values, lengths, allowed):
    scaling = 1.0 / math.sqrt(queries.shape[-1])
    cache_scores = (
        jnp.einsum("rtkgd,rckd->rkgtc", queries, cache_keys, preferred_element_type=jnp.float32)
        * scaling
    )
    tree_scores = (
        jnp.einsum("rtkgd,rskd->rkgts", queries, new_keys, preferred_element_type=jnp.float32)
        * scaling
    )
    live = jnp.arange(cache_keys.shape[1], dtype=jnp.int32)[None, :] < lengths[:, None]
    cache_scores = jnp.where(live[:, None, None, None, :], cache_scores, NEGATIVE)
    tree_scores = jnp.where(allowed[:, None, None, :, :], tree_scores, NEGATIVE)
    highest = jnp.maximum(jnp.max(cache_scores, axis=-1), jnp.max(tree_scores, axis=-1))[..., None]
    cache_exp = jnp.exp(cache_scores - highest)
    tree_exp = jnp.exp(tree_scores - highest)
    denominator = (jnp.sum(cache_exp, axis=-1) + jnp.sum(tree_exp, axis=-1))[..., None]
    cache_probs = (cache_exp / denominator).astype(jnp.bfloat16)
    tree_probs = (tree_exp / denominator).astype(jnp.bfloat16)
    mixed = jnp.einsum(
        "rkgtc,rckd->rtkgd", cache_probs, cache_values, preferred_element_type=jnp.float32
    )
    mixed = mixed + jnp.einsum(
        "rkgts,rskd->rtkgd", tree_probs, new_values, preferred_element_type=jnp.float32
    )
    return mixed.astype(jnp.bfloat16).reshape(queries.shape[0], queries.shape[1], -1)


def shards(
    queries,
    new_keys,
    new_values,
    key_pages,
    value_pages,
    page_table,
    cache_lengths,
    parents,
    residual,
    out_weight,
    norm_gain,
    router_weight,
    routes,
    expert_gate_up,
    expert_down,
    shared_gate_up,
    shared_down,
):
    groups = lax.axis_size("req")
    tp_count = lax.axis_size("tp")
    requests = parents.shape[0]
    tree_size = parents.shape[1]
    row_count = requests * tree_size
    kv_local = new_keys.shape[1] // HD
    head_ratio = QH // KVH
    model_width = residual.shape[1]
    part_width = model_width // tp_count
    pages_dev = key_pages.shape[0]
    local_pages = page_table - lax.axis_index("req") * pages_dev
    cache_keys = key_pages[local_pages].reshape(requests, -1, kv_local, HD)
    cache_values = value_pages[local_pages].reshape(requests, -1, kv_local, HD)
    head_outputs = tree_attention(
        queries.reshape(requests, tree_size, kv_local, head_ratio, HD),
        cache_keys,
        cache_values,
        new_keys.reshape(requests, tree_size, kv_local, HD),
        new_values.reshape(requests, tree_size, kv_local, HD),
        cache_lengths,
        ancestors(parents),
    )
    attn_terms = jnp.dot(
        head_outputs.reshape(row_count, -1), out_weight, preferred_element_type=jnp.float32
    )
    column = lax.axis_index("tp") * part_width
    experts_local = expert_gate_up.shape[0]
    top_count = routes.shape[1]
    expert_count = experts_local * groups
    capacity = max(10 * requests, row_count * top_count * 5 // (4 * expert_count) + 1)
    capacity = -(-capacity // 16) * 16
    slot_count = expert_count * capacity

    flat_expert = routes.reshape(-1)
    expert_ids = jnp.arange(expert_count, dtype=jnp.int32)
    onehot = (flat_expert[:, None] == expert_ids[None, :]).astype(jnp.int32)
    earlier = jnp.cumsum(onehot, axis=0) - onehot
    rank = jnp.sum(earlier * onehot, axis=1)
    slot = (flat_expert * capacity + rank).reshape(row_count, top_count)
    slot_ids = jnp.arange(slot_count, dtype=jnp.int32)
    hit = slot[:, :, None] == slot_ids[None, None, :]

    attn_blocks = attn_terms.astype(jnp.bfloat16).reshape(row_count, tp_count, part_width)
    attn_part = lax.psum_scatter(
        attn_blocks.transpose(1, 0, 2), "tp", scatter_dimension=0, tiled=True
    )[0].astype(jnp.float32)
    residual_part = lax.dynamic_slice_in_dim(residual, column, part_width, 1)
    hidden_part_bf = (residual_part.astype(jnp.float32) + attn_part).astype(jnp.bfloat16)
    hidden_bf = lax.all_gather(hidden_part_bf[None], "tp", axis=0, tiled=True)
    hidden = hidden_bf.transpose(1, 0, 2).reshape(row_count, model_width).astype(jnp.float32)
    rstd = lax.rsqrt(jnp.mean(hidden * hidden, axis=1, keepdims=True) + EPSILON)
    normed = hidden * rstd * norm_gain
    logits = jnp.dot(normed, router_weight, precision=lax.Precision.HIGHEST)
    normed_bf = normed.astype(jnp.bfloat16)
    hidden_part = hidden_part_bf.astype(jnp.float32)

    dispatch = jnp.any(hit, axis=1).astype(jnp.bfloat16)
    dispatch = dispatch.reshape(row_count, groups, experts_local, capacity)
    returns = []
    for expert in range(experts_local):
        outbox = jnp.einsum(
            "tgc,td->gcd", dispatch[:, :, expert], normed_bf, preferred_element_type=jnp.float32
        ).astype(jnp.bfloat16)
        arrived = lax.all_to_all(outbox, "req", split_axis=0, concat_axis=0, tiled=True)
        rows = arrived.reshape(groups * capacity, model_width)
        gate_up = jnp.einsum(
            "md,dcf->mcf", rows, expert_gate_up[expert], preferred_element_type=jnp.float32
        )
        act = (jax.nn.silu(gate_up[:, 0]) * gate_up[:, 1]).astype(jnp.bfloat16)
        partial_value = jnp.dot(act, expert_down[expert], preferred_element_type=jnp.float32)
        partial_bf = partial_value.astype(jnp.bfloat16)
        if expert < experts_local - 1:
            outputs = partial_bf.reshape(groups, capacity, model_width)
        else:
            outputs = lax.psum_scatter(
                partial_bf.reshape(-1, tp_count, part_width).transpose(1, 0, 2),
                "tp", scatter_dimension=0, tiled=True,
            ).reshape(groups, capacity, part_width)
        returns.append(lax.all_to_all(outputs, "req", split_axis=0, concat_axis=0, tiled=True))

    chosen = jnp.sum(
        jnp.where(routes[:, :, None] == expert_ids[None, None, :], logits[:, None, :], 0.0), axis=-1
    )
    gate_values = jax.nn.sigmoid(chosen)
    gate_values = gate_values / jnp.sum(gate_values, axis=1, keepdims=True)
    weights = jnp.sum(jnp.where(hit, gate_values[:, :, None], 0.0), axis=1)
    weights = weights.reshape(row_count, groups, experts_local, capacity)
    weights_hi = weights.astype(jnp.bfloat16)
    weights_lo = (weights - weights_hi.astype(jnp.float32)).astype(jnp.bfloat16)
    weights_split = jnp.stack([weights_hi, weights_lo])
    routed = jnp.zeros((row_count, model_width), jnp.float32)
    for expert in range(experts_local):
        both = jnp.einsum(
            "stgc,gcd->std", weights_split[:, :, :, expert], returns[expert],
            preferred_element_type=jnp.float32,
        )
        if expert < experts_local - 1:
            routed = routed + both[0] + both[1]
        else:
            routed_last = both[0] + both[1]

    shared_gu = jnp.einsum(
        "td,dcf->tcf", normed_bf, shared_gate_up, preferred_element_type=jnp.float32
    )
    shared_act = (jax.nn.silu(shared_gu[:, 0]) * shared_gu[:, 1]).astype(jnp.bfloat16)
    shared_terms = jnp.dot(shared_act, shared_down, preferred_element_type=jnp.float32)
    total = (shared_terms + routed).astype(jnp.bfloat16).reshape(row_count, tp_count, part_width)
    summed = lax.psum_scatter(total.transpose(1, 0, 2), "tp", scatter_dimension=0, tiled=True)
    summed = summed[0].astype(jnp.float32) + routed_last
    return (hidden_part + summed).astype(jnp.bfloat16)


def solution(mesh):
    in_specs = (
        P("req", "tp"),
        P("req", "tp"),
        P("req", "tp"),
        P("req", None, "tp"),
        P("req", None, "tp"),
        P("req", None),
        P("req"),
        P("req", None),
        P("req", None),
        P("tp", None),
        P(),
        P(),
        P("req", None),
        P("req", None, None, "tp"),
        P("req", "tp", None),
        P(None, None, "tp"),
        P("tp", None),
    )
    out_specs = P("req", "tp")
    return jax.shard_map(shards, mesh=mesh, in_specs=in_specs, out_specs=out_specs, check_vma=False)
```

```python
import math

import jax
import jax.numpy as jnp
from jax import lax
from jax.sharding import PartitionSpec as P

QH = 20
KVH = 4
HD = 128


EPSILON = 1e-06
NEGATIVE = -1e30


def rounded(values):
    return lax.optimization_barrier(values.astype(jnp.bfloat16)).astype(jnp.float32)


def ancestors(parents):
    tree_size = parents.shape[-1]
    position = jnp.arange(tree_size, dtype=jnp.int32)
    adjacency = (parents[..., :, None] == position[None, :]) | (
        position[:, None] == position[None, :]
    )
    closure = adjacency.astype(jnp.float32)
    for doubling in range(max(1, (tree_size - 1).bit_length())):
        closure = jnp.minimum(
            jnp.einsum("...ij,...jk->...ik", closure, closure, precision=lax.Precision.HIGHEST), 1.0
        )
    return closure > 0.5


def tree_attention(queries, cache_keys, cache_values, new_keys, new_values, lengths, allowed):
    scaling = 1.0 / math.sqrt(queries.shape[-1])
    cache_scores = (
        jnp.einsum("rtkgd,rckd->rkgtc", queries, cache_keys, preferred_element_type=jnp.float32)
        * scaling
    )
    tree_scores = (
        jnp.einsum("rtkgd,rskd->rkgts", queries, new_keys, preferred_element_type=jnp.float32)
        * scaling
    )
    live = jnp.arange(cache_keys.shape[1], dtype=jnp.int32)[None, :] < lengths[:, None]
    cache_scores = jnp.where(live[:, None, None, None, :], cache_scores, NEGATIVE)
    tree_scores = jnp.where(allowed[:, None, None, :, :], tree_scores, NEGATIVE)
    highest = jnp.maximum(jnp.max(cache_scores, axis=-1), jnp.max(tree_scores, axis=-1))[..., None]
    cache_exp = jnp.exp(cache_scores - highest)
    tree_exp = jnp.exp(tree_scores - highest)
    denominator = (jnp.sum(cache_exp, axis=-1) + jnp.sum(tree_exp, axis=-1))[..., None]
    cache_probs = (cache_exp / denominator).astype(jnp.bfloat16)
    tree_probs = (tree_exp / denominator).astype(jnp.bfloat16)
    mixed = jnp.einsum(
        "rkgtc,rckd->rtkgd", cache_probs, cache_values, preferred_element_type=jnp.float32
    )
    mixed = mixed + jnp.einsum(
        "rkgts,rskd->rtkgd", tree_probs, new_values, preferred_element_type=jnp.float32
    )
    return mixed.astype(jnp.bfloat16).reshape(queries.shape[0], queries.shape[1], -1)


def shards(
    queries,
    new_keys,
    new_values,
    key_pages,
    value_pages,
    page_table,
    cache_lengths,
    parents,
    residual,
    out_weight,
    norm_gain,
    router_weight,
    routes,
    expert_gate_up,
    expert_down,
    shared_gate_up,
    shared_down,
):
    groups = lax.axis_size("req")
    tp_count = lax.axis_size("tp")
    requests = parents.shape[0]
    tree_size = parents.shape[1]
    row_count = requests * tree_size
    kv_local = new_keys.shape[1] // HD
    head_ratio = QH // KVH
    model_width = residual.shape[1]
    part_width = model_width // tp_count
    pages_dev = key_pages.shape[0]
    local_pages = page_table - lax.axis_index("req") * pages_dev
    cache_keys = key_pages[local_pages].reshape(requests, -1, kv_local, HD)
    cache_values = value_pages[local_pages].reshape(requests, -1, kv_local, HD)
    head_outputs = tree_attention(
        queries.reshape(requests, tree_size, kv_local, head_ratio, HD),
        cache_keys,
        cache_values,
        new_keys.reshape(requests, tree_size, kv_local, HD),
        new_values.reshape(requests, tree_size, kv_local, HD),
        cache_lengths,
        ancestors(parents),
    )
    attn_terms = jnp.dot(
        head_outputs.reshape(row_count, -1), out_weight, preferred_element_type=jnp.float32
    )
    column = lax.axis_index("tp") * part_width
    experts_local = expert_gate_up.shape[0]
    top_count = routes.shape[1]
    expert_count = experts_local * groups
    capacity = max(10 * requests, row_count * top_count * 5 // (4 * expert_count) + 1)
    capacity = -(-capacity // 16) * 16
    slot_count = expert_count * capacity

    flat_expert = routes.reshape(-1)
    expert_ids = jnp.arange(expert_count, dtype=jnp.int32)
    onehot = (flat_expert[:, None] == expert_ids[None, :]).astype(jnp.int32)
    earlier = jnp.cumsum(onehot, axis=0) - onehot
    rank = jnp.sum(earlier * onehot, axis=1)
    slot = (flat_expert * capacity + rank).reshape(row_count, top_count)
    slot_ids = jnp.arange(slot_count, dtype=jnp.int32)
    hit = slot[:, :, None] == slot_ids[None, None, :]

    attn_blocks = attn_terms.astype(jnp.bfloat16).reshape(row_count, tp_count, part_width)
    attn_blocks = attn_blocks.transpose(1, 0, 2)
    split_rows = row_count // 2
    attn_first = lax.psum_scatter(
        attn_blocks[:, :split_rows], "tp", scatter_dimension=0, tiled=True
    )[0].astype(jnp.float32)
    attn_second = lax.all_to_all(
        attn_blocks[:, split_rows:], "tp", split_axis=0, concat_axis=0, tiled=True
    )
    attn_second = jnp.sum(attn_second.astype(jnp.float32), axis=0)
    attn_part = jnp.concatenate([attn_first, attn_second], axis=0)
    residual_part = lax.dynamic_slice_in_dim(residual, column, part_width, 1)
    hidden_part_bf = (residual_part.astype(jnp.float32) + attn_part).astype(jnp.bfloat16)
    hidden_bf = lax.all_gather(hidden_part_bf[None], "tp", axis=0, tiled=True)
    hidden = hidden_bf.transpose(1, 0, 2).reshape(row_count, model_width).astype(jnp.float32)
    rstd = lax.rsqrt(jnp.mean(hidden * hidden, axis=1, keepdims=True) + EPSILON)
    normed = hidden * rstd * norm_gain
    logits = jnp.dot(normed, router_weight, precision=lax.Precision.HIGHEST)
    normed_bf = normed.astype(jnp.bfloat16)
    hidden_part = hidden_part_bf.astype(jnp.float32)

    dispatch = jnp.any(hit, axis=1).astype(jnp.bfloat16)
    dispatch = dispatch.reshape(row_count, groups, experts_local, capacity)
    returns = []
    for expert in range(experts_local):
        outbox = jnp.einsum(
            "tgc,td->gcd", dispatch[:, :, expert], normed_bf, preferred_element_type=jnp.float32
        ).astype(jnp.bfloat16)
        arrived = lax.all_to_all(outbox, "req", split_axis=0, concat_axis=0, tiled=True)
        rows = arrived.reshape(groups * capacity, model_width)
        gate_up = jnp.einsum(
            "md,dcf->mcf", rows, expert_gate_up[expert], preferred_element_type=jnp.float32
        )
        act = (jax.nn.silu(gate_up[:, 0]) * gate_up[:, 1]).astype(jnp.bfloat16)
        partial_value = jnp.dot(act, expert_down[expert], preferred_element_type=jnp.float32)
        partial_bf = partial_value.astype(jnp.bfloat16)
        if expert < experts_local - 1:
            outputs = partial_bf.reshape(groups, capacity, model_width)
        else:
            outputs = lax.psum_scatter(
                partial_bf.reshape(-1, tp_count, part_width).transpose(1, 0, 2),
                "tp", scatter_dimension=0, tiled=True,
            ).reshape(groups, capacity, part_width)
        returns.append(lax.all_to_all(outputs, "req", split_axis=0, concat_axis=0, tiled=True))

    chosen = jnp.sum(
        jnp.where(routes[:, :, None] == expert_ids[None, None, :], logits[:, None, :], 0.0), axis=-1
    )
    gate_values = jax.nn.sigmoid(chosen)
    gate_values = gate_values / jnp.sum(gate_values, axis=1, keepdims=True)
    weights = jnp.sum(jnp.where(hit, gate_values[:, :, None], 0.0), axis=1)
    weights = weights.reshape(row_count, groups, experts_local, capacity)
    weights_hi = weights.astype(jnp.bfloat16)
    weights_lo = (weights - weights_hi.astype(jnp.float32)).astype(jnp.bfloat16)
    weights_split = jnp.stack([weights_hi, weights_lo])
    routed = jnp.zeros((row_count, model_width), jnp.float32)
    for expert in range(experts_local):
        both = jnp.einsum(
            "stgc,gcd->std", weights_split[:, :, :, expert], returns[expert],
            preferred_element_type=jnp.float32,
        )
        if expert < experts_local - 1:
            routed = routed + both[0] + both[1]
        else:
            routed_last = both[0] + both[1]

    shared_gu = jnp.einsum(
        "td,dcf->tcf", normed_bf, shared_gate_up, preferred_element_type=jnp.float32
    )
    shared_act = (jax.nn.silu(shared_gu[:, 0]) * shared_gu[:, 1]).astype(jnp.bfloat16)
    shared_terms = jnp.dot(shared_act, shared_down, preferred_element_type=jnp.float32)
    total = (shared_terms + routed).astype(jnp.bfloat16).reshape(row_count, tp_count, part_width)
    summed = lax.psum_scatter(total.transpose(1, 0, 2), "tp", scatter_dimension=0, tiled=True)
    summed = summed[0].astype(jnp.float32) + routed_last
    return (hidden_part + summed).astype(jnp.bfloat16)


def solution(mesh):
    in_specs = (
        P("req", "tp"),
        P("req", "tp"),
        P("req", "tp"),
        P("req", None, "tp"),
        P("req", None, "tp"),
        P("req", None),
        P("req"),
        P("req", None),
        P("req", None),
        P("tp", None),
        P(),
        P(),
        P("req", None),
        P("req", None, None, "tp"),
        P("req", "tp", None),
        P(None, None, "tp"),
        P("tp", None),
    )
    out_specs = P("req", "tp")
    return jax.shard_map(shards, mesh=mesh, in_specs=in_specs, out_specs=out_specs, check_vma=False)
```

```python
import math

import jax
import jax.numpy as jnp
from jax import lax
from jax.sharding import PartitionSpec as P

QH = 20
KVH = 4
HD = 128


EPSILON = 1e-06
NEGATIVE = -1e30


def rounded(values):
    return lax.optimization_barrier(values.astype(jnp.bfloat16)).astype(jnp.float32)


def ancestors(parents):
    tree_size = parents.shape[-1]
    position = jnp.arange(tree_size, dtype=jnp.int32)
    adjacency = (parents[..., :, None] == position[None, :]) | (
        position[:, None] == position[None, :]
    )
    closure = adjacency.astype(jnp.float32)
    for doubling in range(max(1, (tree_size - 1).bit_length())):
        closure = jnp.minimum(
            jnp.einsum("...ij,...jk->...ik", closure, closure, precision=lax.Precision.HIGHEST), 1.0
        )
    return closure > 0.5


def tree_attention(queries, cache_keys, cache_values, new_keys, new_values, lengths, allowed):
    scaling = 1.0 / math.sqrt(queries.shape[-1])
    cache_scores = (
        jnp.einsum("rtkgd,rckd->rkgtc", queries, cache_keys, preferred_element_type=jnp.float32)
        * scaling
    )
    tree_scores = (
        jnp.einsum("rtkgd,rskd->rkgts", queries, new_keys, preferred_element_type=jnp.float32)
        * scaling
    )
    live = jnp.arange(cache_keys.shape[1], dtype=jnp.int32)[None, :] < lengths[:, None]
    cache_scores = jnp.where(live[:, None, None, None, :], cache_scores, NEGATIVE)
    tree_scores = jnp.where(allowed[:, None, None, :, :], tree_scores, NEGATIVE)
    highest = jnp.maximum(jnp.max(cache_scores, axis=-1), jnp.max(tree_scores, axis=-1))[..., None]
    cache_exp = jnp.exp(cache_scores - highest)
    tree_exp = jnp.exp(tree_scores - highest)
    denominator = (jnp.sum(cache_exp, axis=-1) + jnp.sum(tree_exp, axis=-1))[..., None]
    cache_probs = (cache_exp / denominator).astype(jnp.bfloat16)
    tree_probs = (tree_exp / denominator).astype(jnp.bfloat16)
    mixed = jnp.einsum(
        "rkgtc,rckd->rtkgd", cache_probs, cache_values, preferred_element_type=jnp.float32
    )
    mixed = mixed + jnp.einsum(
        "rkgts,rskd->rtkgd", tree_probs, new_values, preferred_element_type=jnp.float32
    )
    return mixed.astype(jnp.bfloat16).reshape(queries.shape[0], queries.shape[1], -1)


def shards(
    queries,
    new_keys,
    new_values,
    key_pages,
    value_pages,
    page_table,
    cache_lengths,
    parents,
    residual,
    out_weight,
    norm_gain,
    router_weight,
    routes,
    expert_gate_up,
    expert_down,
    shared_gate_up,
    shared_down,
):
    groups = lax.axis_size("req")
    tp_count = lax.axis_size("tp")
    requests = parents.shape[0]
    tree_size = parents.shape[1]
    row_count = requests * tree_size
    kv_local = new_keys.shape[1] // HD
    head_ratio = QH // KVH
    model_width = residual.shape[1]
    part_width = model_width // tp_count
    pages_dev = key_pages.shape[0]
    local_pages = page_table - lax.axis_index("req") * pages_dev
    cache_keys = key_pages[local_pages].reshape(requests, -1, kv_local, HD)
    cache_values = value_pages[local_pages].reshape(requests, -1, kv_local, HD)
    head_outputs = tree_attention(
        queries.reshape(requests, tree_size, kv_local, head_ratio, HD),
        cache_keys,
        cache_values,
        new_keys.reshape(requests, tree_size, kv_local, HD),
        new_values.reshape(requests, tree_size, kv_local, HD),
        cache_lengths,
        ancestors(parents),
    )
    attn_terms = jnp.dot(
        head_outputs.reshape(row_count, -1), out_weight, preferred_element_type=jnp.float32
    )
    column = lax.axis_index("tp") * part_width
    experts_local = expert_gate_up.shape[0]
    top_count = routes.shape[1]
    expert_count = experts_local * groups
    capacity = max(10 * requests, row_count * top_count * 5 // (4 * expert_count) + 1)
    capacity = -(-capacity // 16) * 16
    slot_count = expert_count * capacity

    flat_expert = routes.reshape(-1)
    expert_ids = jnp.arange(expert_count, dtype=jnp.int32)
    onehot = (flat_expert[:, None] == expert_ids[None, :]).astype(jnp.int32)
    earlier = jnp.cumsum(onehot, axis=0) - onehot
    rank = jnp.sum(earlier * onehot, axis=1)
    slot = (flat_expert * capacity + rank).reshape(row_count, top_count)
    slot_ids = jnp.arange(slot_count, dtype=jnp.int32)
    hit = slot[:, :, None] == slot_ids[None, None, :]

    attn_blocks = attn_terms.astype(jnp.bfloat16).reshape(row_count, tp_count, part_width)
    attn_part = lax.psum_scatter(
        attn_blocks.transpose(1, 0, 2), "tp", scatter_dimension=0, tiled=True
    )[0].astype(jnp.float32)
    residual_part = lax.dynamic_slice_in_dim(residual, column, part_width, 1)
    hidden_part_bf = (residual_part.astype(jnp.float32) + attn_part).astype(jnp.bfloat16)
    hidden_bf = lax.all_gather(hidden_part_bf[None], "tp", axis=0, tiled=True)
    hidden = hidden_bf.transpose(1, 0, 2).reshape(row_count, model_width).astype(jnp.float32)
    rstd = lax.rsqrt(jnp.mean(hidden * hidden, axis=1, keepdims=True) + EPSILON)
    normed = hidden * rstd * norm_gain
    logits = jnp.dot(normed, router_weight, precision=lax.Precision.HIGHEST)
    normed_bf = normed.astype(jnp.bfloat16)
    hidden_part = hidden_part_bf.astype(jnp.float32)

    dispatch = jnp.any(slot_ids[:, None, None] == slot[None, :, :], axis=2).astype(jnp.bfloat16)
    dispatch = dispatch.reshape(groups, experts_local, capacity, row_count)
    returns = []
    for expert in range(experts_local):
        outbox = jnp.einsum(
            "gct,td->gcd", dispatch[:, expert], normed_bf, preferred_element_type=jnp.float32
        ).astype(jnp.bfloat16)
        arrived = lax.all_to_all(outbox, "req", split_axis=0, concat_axis=0, tiled=True)
        rows = arrived.reshape(groups * capacity, model_width)
        gate_up = jnp.einsum(
            "md,dcf->mcf", rows, expert_gate_up[expert], preferred_element_type=jnp.float32
        )
        act = (jax.nn.silu(gate_up[:, 0]) * gate_up[:, 1]).astype(jnp.bfloat16)
        partial_value = jnp.dot(act, expert_down[expert], preferred_element_type=jnp.float32)
        partial_bf = partial_value.astype(jnp.bfloat16)
        if expert < experts_local - 1:
            outputs = partial_bf.reshape(groups, capacity, model_width)
        else:
            outputs = lax.psum_scatter(
                partial_bf.reshape(-1, tp_count, part_width).transpose(1, 0, 2),
                "tp", scatter_dimension=0, tiled=True,
            ).reshape(groups, capacity, part_width)
        returns.append(lax.all_to_all(outputs, "req", split_axis=0, concat_axis=0, tiled=True))

    chosen = jnp.sum(
        jnp.where(routes[:, :, None] == expert_ids[None, None, :], logits[:, None, :], 0.0), axis=-1
    )
    gate_values = jax.nn.sigmoid(chosen)
    gate_values = gate_values / jnp.sum(gate_values, axis=1, keepdims=True)
    weights = jnp.sum(jnp.where(hit, gate_values[:, :, None], 0.0), axis=1)
    weights = weights.reshape(row_count, groups, experts_local, capacity)
    weights_hi = weights.astype(jnp.bfloat16)
    weights_lo = (weights - weights_hi.astype(jnp.float32)).astype(jnp.bfloat16)
    weights_split = jnp.stack([weights_hi, weights_lo])
    routed = jnp.zeros((row_count, model_width), jnp.float32)
    for expert in range(experts_local):
        both = jnp.einsum(
            "stgc,gcd->std", weights_split[:, :, :, expert], returns[expert],
            preferred_element_type=jnp.float32,
        )
        if expert < experts_local - 1:
            routed = routed + both[0] + both[1]
        else:
            routed_last = both[0] + both[1]

    shared_gu = jnp.einsum(
        "td,dcf->tcf", normed_bf, shared_gate_up, preferred_element_type=jnp.float32
    )
    shared_act = (jax.nn.silu(shared_gu[:, 0]) * shared_gu[:, 1]).astype(jnp.bfloat16)
    shared_terms = jnp.dot(shared_act, shared_down, preferred_element_type=jnp.float32)
    total = (shared_terms + routed).astype(jnp.bfloat16).reshape(row_count, tp_count, part_width)
    summed = lax.psum_scatter(total.transpose(1, 0, 2), "tp", scatter_dimension=0, tiled=True)
    summed = summed[0].astype(jnp.float32) + routed_last
    return (hidden_part + summed).astype(jnp.bfloat16)


def solution(mesh):
    in_specs = (
        P("req", "tp"),
        P("req", "tp"),
        P("req", "tp"),
        P("req", None, "tp"),
        P("req", None, "tp"),
        P("req", None),
        P("req"),
        P("req", None),
        P("req", None),
        P("tp", None),
        P(),
        P(),
        P("req", None),
        P("req", None, None, "tp"),
        P("req", "tp", None),
        P(None, None, "tp"),
        P("tp", None),
    )
    out_specs = P("req", "tp")
    return jax.shard_map(shards, mesh=mesh, in_specs=in_specs, out_specs=out_specs, check_vma=False)
```

```python
import math

import jax
import jax.numpy as jnp
from jax import lax
from jax.sharding import PartitionSpec as P

QH = 20
KVH = 4
HD = 128


EPSILON = 1e-06
NEGATIVE = -1e30


def rounded(values):
    return lax.optimization_barrier(values.astype(jnp.bfloat16)).astype(jnp.float32)


def ancestors(parents):
    tree_size = parents.shape[-1]
    position = jnp.arange(tree_size, dtype=jnp.int32)
    adjacency = (parents[..., :, None] == position[None, :]) | (
        position[:, None] == position[None, :]
    )
    closure = adjacency.astype(jnp.float32)
    for doubling in range(max(1, (tree_size - 1).bit_length())):
        closure = jnp.minimum(
            jnp.einsum("...ij,...jk->...ik", closure, closure, precision=lax.Precision.HIGHEST), 1.0
        )
    return closure > 0.5


def tree_attention(queries, cache_keys, cache_values, new_keys, new_values, lengths, allowed):
    scaling = 1.0 / math.sqrt(queries.shape[-1])
    cache_scores = (
        jnp.einsum("rtkgd,rckd->rkgtc", queries, cache_keys, preferred_element_type=jnp.float32)
        * scaling
    )
    tree_scores = (
        jnp.einsum("rtkgd,rskd->rkgts", queries, new_keys, preferred_element_type=jnp.float32)
        * scaling
    )
    live = jnp.arange(cache_keys.shape[1], dtype=jnp.int32)[None, :] < lengths[:, None]
    cache_scores = jnp.where(live[:, None, None, None, :], cache_scores, NEGATIVE)
    tree_scores = jnp.where(allowed[:, None, None, :, :], tree_scores, NEGATIVE)
    highest = jnp.maximum(jnp.max(cache_scores, axis=-1), jnp.max(tree_scores, axis=-1))[..., None]
    cache_exp = jnp.exp(cache_scores - highest)
    tree_exp = jnp.exp(tree_scores - highest)
    denominator = (jnp.sum(cache_exp, axis=-1) + jnp.sum(tree_exp, axis=-1))[..., None]
    cache_probs = (cache_exp / denominator).astype(jnp.bfloat16)
    tree_probs = (tree_exp / denominator).astype(jnp.bfloat16)
    mixed = jnp.einsum(
        "rkgtc,rckd->rtkgd", cache_probs, cache_values, preferred_element_type=jnp.float32
    )
    mixed = mixed + jnp.einsum(
        "rkgts,rskd->rtkgd", tree_probs, new_values, preferred_element_type=jnp.float32
    )
    return mixed.astype(jnp.bfloat16).reshape(queries.shape[0], queries.shape[1], -1)


def shards(
    queries,
    new_keys,
    new_values,
    key_pages,
    value_pages,
    page_table,
    cache_lengths,
    parents,
    residual,
    out_weight,
    norm_gain,
    router_weight,
    routes,
    expert_gate_up,
    expert_down,
    shared_gate_up,
    shared_down,
):
    groups = lax.axis_size("req")
    tp_count = lax.axis_size("tp")
    requests = parents.shape[0]
    tree_size = parents.shape[1]
    row_count = requests * tree_size
    kv_local = new_keys.shape[1] // HD
    head_ratio = QH // KVH
    model_width = residual.shape[1]
    part_width = model_width // tp_count
    pages_dev = key_pages.shape[0]
    local_pages = page_table - lax.axis_index("req") * pages_dev
    cache_keys = key_pages[local_pages].reshape(requests, -1, kv_local, HD)
    cache_values = value_pages[local_pages].reshape(requests, -1, kv_local, HD)
    head_outputs = tree_attention(
        queries.reshape(requests, tree_size, kv_local, head_ratio, HD),
        cache_keys,
        cache_values,
        new_keys.reshape(requests, tree_size, kv_local, HD),
        new_values.reshape(requests, tree_size, kv_local, HD),
        cache_lengths,
        ancestors(parents),
    )
    attn_terms = jnp.einsum(
        "tk,kzd->ztd", head_outputs.reshape(row_count, -1),
        out_weight.reshape(out_weight.shape[0], tp_count, -1), preferred_element_type=jnp.float32,
    )
    column = lax.axis_index("tp") * part_width
    experts_local = expert_gate_up.shape[0]
    top_count = routes.shape[1]
    expert_count = experts_local * groups
    capacity = max(10 * requests, row_count * top_count * 5 // (4 * expert_count) + 1)
    capacity = -(-capacity // 16) * 16
    slot_count = expert_count * capacity

    flat_expert = routes.reshape(-1)
    expert_ids = jnp.arange(expert_count, dtype=jnp.int32)
    onehot = (flat_expert[:, None] == expert_ids[None, :]).astype(jnp.int32)
    earlier = jnp.cumsum(onehot, axis=0) - onehot
    rank = jnp.sum(earlier * onehot, axis=1)
    slot = (flat_expert * capacity + rank).reshape(row_count, top_count)
    slot_ids = jnp.arange(slot_count, dtype=jnp.int32)
    hit = slot[:, :, None] == slot_ids[None, None, :]

    attn_blocks = attn_terms.astype(jnp.bfloat16)
    attn_part = lax.psum_scatter(
        attn_blocks, "tp", scatter_dimension=0, tiled=True
    )[0].astype(jnp.float32)
    residual_part = lax.dynamic_slice_in_dim(residual, column, part_width, 1)
    hidden_part_bf = (residual_part.astype(jnp.float32) + attn_part).astype(jnp.bfloat16)
    hidden_bf = lax.all_gather(hidden_part_bf[None], "tp", axis=0, tiled=True)
    hidden = hidden_bf.transpose(1, 0, 2).reshape(row_count, model_width).astype(jnp.float32)
    rstd = lax.rsqrt(jnp.mean(hidden * hidden, axis=1, keepdims=True) + EPSILON)
    normed = hidden * rstd * norm_gain
    logits = jnp.dot(normed, router_weight, precision=lax.Precision.HIGHEST)
    normed_bf = normed.astype(jnp.bfloat16)
    hidden_part = hidden_part_bf.astype(jnp.float32)

    dispatch = jnp.any(hit, axis=1).astype(jnp.bfloat16)
    dispatch = dispatch.reshape(row_count, groups, experts_local, capacity)
    returns = []
    for expert in range(experts_local):
        outbox = jnp.einsum(
            "tgc,td->gcd", dispatch[:, :, expert], normed_bf, preferred_element_type=jnp.float32
        ).astype(jnp.bfloat16)
        arrived = lax.all_to_all(outbox, "req", split_axis=0, concat_axis=0, tiled=True)
        rows = arrived.reshape(groups * capacity, model_width)
        gate_up = jnp.einsum(
            "md,dcf->mcf", rows, expert_gate_up[expert], preferred_element_type=jnp.float32
        )
        act = (jax.nn.silu(gate_up[:, 0]) * gate_up[:, 1]).astype(jnp.bfloat16)
        partial_value = jnp.dot(act, expert_down[expert], preferred_element_type=jnp.float32)
        partial_bf = partial_value.astype(jnp.bfloat16)
        if expert < experts_local - 1:
            outputs = partial_bf.reshape(groups, capacity, model_width)
        else:
            outputs = lax.psum_scatter(
                partial_bf.reshape(-1, tp_count, part_width).transpose(1, 0, 2),
                "tp", scatter_dimension=0, tiled=True,
            ).reshape(groups, capacity, part_width)
        returns.append(lax.all_to_all(outputs, "req", split_axis=0, concat_axis=0, tiled=True))

    chosen = jnp.sum(
        jnp.where(routes[:, :, None] == expert_ids[None, None, :], logits[:, None, :], 0.0), axis=-1
    )
    gate_values = jax.nn.sigmoid(chosen)
    gate_values = gate_values / jnp.sum(gate_values, axis=1, keepdims=True)
    weights = jnp.sum(jnp.where(hit, gate_values[:, :, None], 0.0), axis=1)
    weights = weights.reshape(row_count, groups, experts_local, capacity)
    weights_hi = weights.astype(jnp.bfloat16)
    weights_lo = (weights - weights_hi.astype(jnp.float32)).astype(jnp.bfloat16)
    weights_split = jnp.stack([weights_hi, weights_lo])
    routed = jnp.zeros((row_count, model_width), jnp.float32)
    for expert in range(experts_local):
        both = jnp.einsum(
            "stgc,gcd->std", weights_split[:, :, :, expert], returns[expert],
            preferred_element_type=jnp.float32,
        )
        if expert < experts_local - 1:
            routed = routed + both[0] + both[1]
        else:
            routed_last = both[0] + both[1]

    shared_gu = jnp.einsum(
        "td,dcf->tcf", normed_bf, shared_gate_up, preferred_element_type=jnp.float32
    )
    shared_act = (jax.nn.silu(shared_gu[:, 0]) * shared_gu[:, 1]).astype(jnp.bfloat16)
    shared_terms = jnp.dot(shared_act, shared_down, preferred_element_type=jnp.float32)
    total = (shared_terms + routed).astype(jnp.bfloat16).reshape(row_count, tp_count, part_width)
    summed = lax.psum_scatter(total.transpose(1, 0, 2), "tp", scatter_dimension=0, tiled=True)
    summed = summed[0].astype(jnp.float32) + routed_last
    return (hidden_part + summed).astype(jnp.bfloat16)


def solution(mesh):
    in_specs = (
        P("req", "tp"),
        P("req", "tp"),
        P("req", "tp"),
        P("req", None, "tp"),
        P("req", None, "tp"),
        P("req", None),
        P("req"),
        P("req", None),
        P("req", None),
        P("tp", None),
        P(),
        P(),
        P("req", None),
        P("req", None, None, "tp"),
        P("req", "tp", None),
        P(None, None, "tp"),
        P("tp", None),
    )
    out_specs = P("req", "tp")
    return jax.shard_map(shards, mesh=mesh, in_specs=in_specs, out_specs=out_specs, check_vma=False)
```
